128 devices in a mesh: leaf: 128 (over y, x, z, core).
Axes of the slice: x: 4, y: 4, z: 4, core: 2. Of those that a mesh axis runs over, the one named last changes fastest.
Arguments:
- values: bfloat16 [32768, 8, 128], P('leaf'), may hold values from -6 to 6
- points: bfloat16 [32768, 2, 128], P('leaf'), may hold values from 0 to 6
- basis: bfloat16 [32768, 64, 128], P('leaf'), may hold values from -0.5 to 0.5
- leaf_up: bfloat16 [32768, 4096], P('leaf'), may hold values from -0.5 to 0.5
- mid_up: bfloat16 [8192, 4096], P('leaf'), may hold values from -0.5 to 0.5
- box_up: bfloat16 [2048, 4096], P('leaf'), may hold values from -0.5 to 0.5
- leaf_skel: bfloat16 [32768, 128], P('leaf'), may hold values from 0 to 6
- mid_skel: bfloat16 [8192, 128], P('leaf'), may hold values from 0 to 6
- box_skel: bfloat16 [2048, 128], P('leaf'), may hold values from 0 to 6
- top_skel: bfloat16 [512, 128], replicated, may hold values from 0 to 6
- near_src: int32 [32768, 9], P('leaf'), may hold values from 0 to 32767, as said below
- near_count: int32 [32768], P('leaf'), may hold values from 1 to 9
- leaf_src: int32 [32768, 27], P('leaf'), may hold values from 0 to 32767, as said below
- leaf_count: int32 [32768], P('leaf'), may hold values from 1 to 27
- mid_src: int32 [8192, 27], P('leaf'), may hold values from 0 to 8191, as said below
- mid_count: int32 [8192], P('leaf'), may hold values from 1 to 27
- box_src: int32 [2048, 27], P('leaf'), may hold values from 0 to 2047, as said below
- box_count: int32 [2048], P('leaf'), may hold values from 1 to 27
- box_parent: int32 [2048], replicated, may hold values from 0 to 511, as said below
- top_src: int32 [512, 27], P('leaf'), may hold values from 0 to 511
- top_count: int32 [512], P('leaf'), may hold values from 1 to 27
Outputs:
- potential: float32 [32768, 8, 128], P('leaf')
The draws below stay inside these ranges and needn't reach their ends.
Inputs may be any that keep to these rules, and one draw needn't show every extreme that they name: `near_src`: every entry of a leaf's list lies on the device of that leaf or on one of the two beside it along leaf; slots past the count hold valid indices too. `leaf_src`: every entry lies on the device of its node or on one of the two beside it along leaf. `mid_src`: every entry lies on the device of its node or on one of the two beside it along leaf. `box_src`: every entry lies on the device of its node or on one of the two beside it along leaf. `box_parent`: every top node is the parent of exactly four level-two nodes, and these are the boxes 4k .. 4k + 3 for some k, all held on one device.
All inputs are finite; a program needn't handle non-finite values.
Results may differ from the reference program's by a relative error of at most 0.0095.
Values may be sent and summed in bfloat16 or wider, within the bound.
No kernel may reach another device: no remote copies, remote signals or barrier semaphores. Data moves between devices by JAX's collectives and lax.ppermute only.
A program may use at most 64 MiB of HBM per device.

```python
import jax
import jax.numpy as jnp
from jax import lax

P_SIZE = 128
R = 64
S = 8
KN = 9
KF = 27
LEAF_DEV = 256
LEAVES = 32768
MIDS = 8192
BOXES = 2048
TOP = 512


def neighbour_lists(key, nodes, per_device, slots):
    row_ids = jnp.arange(nodes, dtype=jnp.int32)[:, None]
    offsets = jax.random.randint(key, (nodes, slots), -per_device, per_device + 1, dtype=jnp.int32)
    return jnp.clip(row_ids + offsets, 0, nodes - 1).astype(jnp.int32)


def skewed_counts(key, nodes, per_device, most):
    devices = nodes // per_device
    first, second, third, fourth = jax.random.split(key, 4)
    divisor = jax.random.randint(first, (devices,), 1, 5, dtype=jnp.int32)
    density = jnp.maximum(most // divisor, 2)
    density = density.at[jax.random.randint(second, (), 0, devices, dtype=jnp.int32)].set(most)
    counts = jax.random.randint(third, (devices, per_device), 1, density[:, None] + 1, dtype=jnp.int32)
    position = jax.random.randint(fourth, (devices,), 0, per_device, dtype=jnp.int32)
    counts = jnp.where(jnp.arange(per_device, dtype=jnp.int32)[None, :] == position[:, None], density[:, None], counts)
    return counts.reshape(nodes).astype(jnp.int32)


def draw_near_src(key, part):
    return neighbour_lists(jax.random.fold_in(key, 101), LEAVES, LEAF_DEV, KN)


def draw_near_count(key, part):
    return skewed_counts(jax.random.fold_in(key, 102), LEAVES, LEAF_DEV, KN)


def draw_leaf_src(key, part):
    return neighbour_lists(jax.random.fold_in(key, 103), LEAVES, LEAF_DEV, KF)


def draw_leaf_count(key, part):
    return skewed_counts(jax.random.fold_in(key, 104), LEAVES, LEAF_DEV, KF)


def draw_mid_src(key, part):
    return neighbour_lists(jax.random.fold_in(key, 105), MIDS, LEAF_DEV // 4, KF)


def draw_mid_count(key, part):
    return skewed_counts(jax.random.fold_in(key, 106), MIDS, LEAF_DEV // 4, KF)


def draw_box_src(key, part):
    return neighbour_lists(jax.random.fold_in(key, 107), BOXES, LEAF_DEV // 16, KF)


def draw_box_count(key, part):
    return skewed_counts(jax.random.fold_in(key, 108), BOXES, LEAF_DEV // 16, KF)


def draw_top_count(key, part):
    return skewed_counts(jax.random.fold_in(key, 109), TOP, LEAF_DEV // 64, KF)


def draw_box_parent(key, part):
    order = jax.random.permutation(jax.random.fold_in(key, 110), TOP).astype(jnp.int32)
    return order[jnp.arange(BOXES, dtype=jnp.int32) // 4].astype(jnp.int32)


def with_ends(array, rng, least, high):
    longest = array.shape.index(max(array.shape))
    spots = []
    for shift in (0, 1):
        where = [jax.random.randint(jax.random.fold_in(rng, axis), (), 0, length) for axis, length in enumerate(array.shape)]
        where[longest] = (where[longest] + shift) % array.shape[longest]
        spots.append(tuple(where))
    return array.at[spots[0]].set(least).at[spots[1]].set(high)


def levels(own_key, extent, pieces, low, largest):
    loudness = 1.0
    for dim, shards_of in pieces:
        draws = jax.random.uniform(jax.random.fold_in(jax.random.fold_in(own_key, 6), dim), (shards_of,), jnp.float32, low / len(pieces), largest / len(pieces))
        loudness = loudness * jnp.repeat(jnp.exp(draws), extent[dim] // shards_of).reshape((-1,) + (1,) * (len(extent) - 1 - dim))
    return loudness


def gaussian(own_key, shape, deviation, limit, cuts=(), kind=jnp.bfloat16):
    array = jax.random.normal(own_key, shape, jnp.float32) * deviation
    if len(cuts) > 0:
        array = levels(own_key, shape, cuts, -0.22, 0.18) * array
    return jnp.clip(array, min=-limit, max=limit).astype(kind)


def setup_inputs(seed: int = 0) -> dict:
    splits = jax.random.split(jax.random.key(seed), 22)
    values = gaussian(splits[0], (LEAVES, S, P_SIZE), 1.0, 6.0, ((0, 128),))
    points = jnp.clip(6.0 * jax.random.uniform(splits[1], (LEAVES, 2, P_SIZE), jnp.float32) ** levels(splits[1], (LEAVES, 2, P_SIZE), ((0, 128),), -0.2, 0.2), 0.0, 6.0).astype(jnp.bfloat16)
    basis = gaussian(splits[2], (LEAVES, R, P_SIZE), P_SIZE ** -0.5, 0.5, ((0, 128),))
    leaf_up = gaussian(splits[3], (LEAVES, R * R), (2 * R) ** -0.5, 0.5, ((0, 128),))
    mid_up = gaussian(splits[4], (MIDS, R * R), (2 * R) ** -0.5, 0.5, ((0, 128),))
    box_up = gaussian(splits[5], (BOXES, R * R), (2 * R) ** -0.5, 0.5, ((0, 128),))
    leaf_skel = jnp.clip(6.0 * jax.random.uniform(splits[6], (LEAVES, 2 * R), jnp.float32) ** levels(splits[6], (LEAVES, 2 * R), ((0, 128),), -0.2, 0.2), 0.0, 6.0).astype(jnp.bfloat16)
    mid_skel = jnp.clip(6.0 * jax.random.uniform(splits[7], (MIDS, 2 * R), jnp.float32) ** levels(splits[7], (MIDS, 2 * R), ((0, 128),), -0.2, 0.2), 0.0, 6.0).astype(jnp.bfloat16)
    box_skel = jnp.clip(6.0 * jax.random.uniform(splits[8], (BOXES, 2 * R), jnp.float32) ** levels(splits[8], (BOXES, 2 * R), ((0, 128),), -0.2, 0.2), 0.0, 6.0).astype(jnp.bfloat16)
    top_skel = jnp.clip(jax.random.uniform(splits[9], (TOP, 2 * R), jnp.float32, 0.0, 6.0), 0.0, 6.0).astype(jnp.bfloat16)
    near_src = draw_near_src(jax.random.fold_in(splits[21], 71), 0)
    near_count = draw_near_count(jax.random.fold_in(splits[21], 71), 0)
    leaf_src = draw_leaf_src(jax.random.fold_in(splits[21], 71), 0)
    leaf_count = draw_leaf_count(jax.random.fold_in(splits[21], 71), 0)
    mid_src = draw_mid_src(jax.random.fold_in(splits[21], 71), 0)
    mid_count = draw_mid_count(jax.random.fold_in(splits[21], 71), 0)
    box_src = draw_box_src(jax.random.fold_in(splits[21], 71), 0)
    box_count = draw_box_count(jax.random.fold_in(splits[21], 71), 0)
    box_parent = draw_box_parent(jax.random.fold_in(splits[21], 71), 0)
    top_src = with_ends(jax.random.randint(splits[19], (TOP, KF), 0, TOP), jax.random.fold_in(splits[19], 1), 0, TOP - 1).astype(jnp.int32)
    top_count = draw_top_count(jax.random.fold_in(splits[21], 71), 0)
    return {"values": values, "points": points, "basis": basis, "leaf_up": leaf_up, "mid_up": mid_up, "box_up": box_up, "leaf_skel": leaf_skel, "mid_skel": mid_skel, "box_skel": box_skel, "top_skel": top_skel, "near_src": near_src, "near_count": near_count, "leaf_src": leaf_src, "leaf_count": leaf_count, "mid_src": mid_src, "mid_count": mid_count, "box_src": box_src, "box_count": box_count, "box_parent": box_parent, "top_src": top_src, "top_count": top_count}


def kernel_tile(targets, sources):
    first = targets.astype(jnp.float32)
    second = sources.astype(jnp.float32)
    delta_x = first[:, 0, :, None] - second[:, 0, None, :]
    delta_y = first[:, 1, :, None] - second[:, 1, None, :]
    return (0.25 * jnp.exp(-jnp.sqrt(delta_x * delta_x + delta_y * delta_y + 0.0025))).astype(jnp.bfloat16)

def near_sum(values, points, sources, counts, block_size):
    leaves = values.shape[0]

    def one_block(number):
        first_row = (number * block_size).astype(jnp.int32)
        targets = lax.dynamic_slice_in_dim(points, first_row, block_size)
        source_ids = lax.dynamic_slice_in_dim(sources, first_row, block_size)
        live_count = lax.dynamic_slice_in_dim(counts, first_row, block_size)
        running = jnp.zeros((block_size, S, P_SIZE), jnp.float32)
        for column in range(sources.shape[1]):
            picked = source_ids[:, column]
            coupling = kernel_tile(targets, points[picked])
            contrib = jnp.einsum('bsq,bpq->bsp', values[picked].astype(jnp.float32), coupling.astype(jnp.float32))
            running = running + jnp.where((column < live_count)[:, None, None], contrib, 0.0)
        return running
    blocks = lax.map(one_block, jnp.arange(leaves // block_size, dtype=jnp.int32))
    return blocks.reshape(leaves, S, P_SIZE)

def far_sum(coeffs, skeleton, sources, counts, block_size):
    nodes = coeffs.shape[0]
    frames = skeleton.reshape(nodes, 2, R)

    def one_block(number):
        first_row = (number * block_size).astype(jnp.int32)
        targets = lax.dynamic_slice_in_dim(frames, first_row, block_size)
        source_ids = lax.dynamic_slice_in_dim(sources, first_row, block_size)
        live_count = lax.dynamic_slice_in_dim(counts, first_row, block_size)
        running = jnp.zeros((block_size, S, R), jnp.float32)
        for column in range(sources.shape[1]):
            picked = source_ids[:, column]
            coupling = kernel_tile(targets, frames[picked])
            contrib = jnp.einsum('nsq,nrq->nsr', coeffs[picked].astype(jnp.float32), coupling.astype(jnp.float32))
            running = running + jnp.where((column < live_count)[:, None, None], contrib, 0.0)
        return running
    blocks = lax.map(one_block, jnp.arange(nodes // block_size, dtype=jnp.int32))
    return blocks.reshape(nodes, S, R)

def lift_up(coeffs, transfer):
    nodes = coeffs.shape[0]
    matrices = transfer.reshape(nodes, R, R).astype(jnp.float32)
    return jnp.einsum('nsq,nqr->nsr', coeffs.astype(jnp.float32), matrices)

def reference(values, points, basis, leaf_up, mid_up, box_up, leaf_skel, mid_skel, box_skel, top_skel, near_src, near_count, leaf_src, leaf_count, mid_src, mid_count, box_src, box_count, box_parent, top_src, top_count):
    near_field = near_sum(values, points, near_src, near_count, LEAF_DEV)
    leaf_coef = jnp.einsum('tsp,trp->tsr', values.astype(jnp.float32), basis.astype(jnp.float32)).astype(jnp.bfloat16)
    mid_coef = lift_up(leaf_coef, leaf_up).reshape(-1, 4, S, R).sum(axis=1).astype(jnp.bfloat16)
    box_coef = lift_up(mid_coef, mid_up).reshape(-1, 4, S, R).sum(axis=1).astype(jnp.bfloat16)
    box_term = lift_up(box_coef, box_up).astype(jnp.bfloat16)
    top_coef = jax.ops.segment_sum(box_term.astype(jnp.float32), box_parent, num_segments=TOP).astype(jnp.bfloat16)
    leaf_far = far_sum(leaf_coef, leaf_skel, leaf_src, leaf_count, LEAF_DEV)
    mid_far = far_sum(mid_coef, mid_skel, mid_src, mid_count, LEAF_DEV // 4)
    box_far = far_sum(box_coef, box_skel, box_src, box_count, LEAF_DEV // 16)
    top_field = far_sum(top_coef, top_skel, top_src, top_count, TOP).astype(jnp.bfloat16)
    box_field = (box_far + jnp.einsum('bsr,bqr->bsq', top_field[box_parent].astype(jnp.float32), box_up.reshape(-1, R, R).astype(jnp.float32))).astype(jnp.bfloat16)
    mid_field = (mid_far + jnp.einsum('bsr,bjqr->bjsq', box_field.astype(jnp.float32), mid_up.reshape(-1, 4, R, R).astype(jnp.float32)).reshape(-1, S, R)).astype(jnp.bfloat16)
    leaf_field = (leaf_far + jnp.einsum('bsr,bjqr->bjsq', mid_field.astype(jnp.float32), leaf_up.reshape(-1, 4, R, R).astype(jnp.float32)).reshape(-1, S, R)).astype(jnp.bfloat16)
    return near_field + jnp.einsum('tsr,trp->tsp', leaf_field.astype(jnp.float32), basis.astype(jnp.float32))
```

```python
import functools

import jax
import jax.numpy as jnp
from jax import lax
from jax.experimental import pallas as pl
from jax.experimental.pallas import tpu as pltpu
from jax.sharding import PartitionSpec as P


def padded(shard, sides, width):
    for axis, dim in sides:
        size, length = (lax.axis_size(axis), shard.shape[dim])
        up = [(i, (i + 1) % size) for i in range(size - 1)]
        down = [(j, i) for i, j in up]
        last = lax.slice_in_dim(shard, length - width, length, axis=dim)
        leading = lax.slice_in_dim(shard, 0, width, axis=dim)
        before = lax.ppermute(last, axis, up)
        after = lax.ppermute(leading, axis, down)
        shard = jnp.concatenate([before, shard, after], axis=dim)
    return shard


def lift_up(coeffs, transfer, rank_width):
    nodes = coeffs.shape[0]
    matrices = transfer.reshape(nodes, rank_width, rank_width)
    return jnp.einsum("nsq,nqr->nsr", coeffs, matrices, preferred_element_type=jnp.float32)


def column_broadcast(row):
    width = row.shape[1]
    return jnp.transpose(jnp.broadcast_to(row, (width, width)))


def coupling(dx, dy):
    return jnp.exp(-jnp.sqrt(dx * dx + dy * dy + 0.0025)).astype(jnp.bfloat16)


def near_kernel(base_ref, src_ref, cnt_ref, vals_ref, pts_ref, out_ref, *, slots):
    targets = out_ref.shape[0]
    base = base_ref[0]

    def per_target(t, carry):
        own = pts_ref[pl.ds(2 * (base + t), 2), :]
        tx = column_broadcast(own[0:1, :])
        ty = column_broadcast(own[1:2, :])

        def slot(j, acc):
            s = src_ref[t * slots + j]
            sp = pts_ref[pl.ds(2 * s, 2), :]
            k = coupling(tx - sp[0:1, :], ty - sp[1:2, :])
            v = vals_ref[s]
            return acc + lax.dot_general(
                k, v, (((1,), (1,)), ((), ())), preferred_element_type=jnp.float32
            )

        acc = lax.fori_loop(0, cnt_ref[t], slot, jnp.zeros((own.shape[1], v_rows), jnp.float32))
        out_ref[t] = jnp.transpose(0.25 * acc)
        return carry

    v_rows = vals_ref.shape[1]
    lax.fori_loop(0, targets, per_target, 0)


def far_kernel(base_ref, src_ref, cnt_ref, cd_ref, sk_ref, sw_ref, out_ref, *, slots):
    targets, rows, rank = out_ref.shape
    width = sk_ref.shape[1]
    base = base_ref[0]
    first_half = lax.broadcasted_iota(jnp.int32, (1, width), 1) < rank
    first_half_c = lax.broadcasted_iota(jnp.int32, (rows, width), 1) < rank
    zeros_c = jnp.zeros((rows, width), cd_ref.dtype)

    def per_target(t, carry):
        own = sk_ref[pl.ds(base + t, 1), :]
        frame = column_broadcast(own)
        tx = frame[:rank]
        ty = frame[rank:]
        count = cnt_ref[t]

        def slot(i, acc):
            j = 2 * i
            s1 = src_ref[t * slots + j]
            s2 = src_ref[t * slots + jnp.minimum(j + 1, slots - 1)]
            sx = jnp.where(first_half, sk_ref[pl.ds(s1, 1), :], sw_ref[pl.ds(s2, 1), :])
            sy = jnp.where(first_half, sw_ref[pl.ds(s1, 1), :], sk_ref[pl.ds(s2, 1), :])
            k = coupling(tx - sx, ty - sy)
            c2 = jnp.where(j + 1 < count, cd_ref[s2], zeros_c)
            cm = jnp.where(first_half_c, cd_ref[s1], c2)
            return acc + lax.dot_general(
                k, cm, (((1,), (1,)), ((), ())), preferred_element_type=jnp.float32
            )

        acc = lax.fori_loop(0, (count + 1) // 2, slot, jnp.zeros((rank, rows), jnp.float32))
        out_ref[t] = jnp.transpose(0.25 * acc)
        return carry

    lax.fori_loop(0, targets, per_target, 0)


SMEM = pl.BlockSpec(memory_space=pltpu.SMEM)
VMEM = pl.BlockSpec(memory_space=pltpu.VMEM)


def near_sum(base, src, counts, vals, pts):
    targets, slots = src.shape
    rows, width = vals.shape[1], vals.shape[2]
    tile = width * width
    pairs = targets * slots
    return pl.pallas_call(
        functools.partial(near_kernel, slots=slots),
        out_shape=jax.ShapeDtypeStruct((targets, rows, width), jnp.float32),
        in_specs=[SMEM, SMEM, SMEM, VMEM, VMEM],
        out_specs=VMEM,
        compiler_params=pltpu.CompilerParams(vmem_limit_bytes=48 * 1024 * 1024),
        cost_estimate=pl.CostEstimate(
            flops=pairs * (2 * rows * tile + 10 * tile),
            transcendentals=pairs * 2 * tile,
            bytes_accessed=vals.size * 2 + pts.size * 4 + targets * rows * width * 4,
        ),
    )(base, src.reshape(-1), counts, vals, pts)


def far_sum(base, src, counts, cd, sk, sw, rank):
    targets, slots = src.shape
    rows, width = cd.shape[1], cd.shape[2]
    tile = rank * width
    pairs = targets * (slots + 1) // 2
    return pl.pallas_call(
        functools.partial(far_kernel, slots=slots),
        out_shape=jax.ShapeDtypeStruct((targets, rows, rank), jnp.float32),
        in_specs=[SMEM, SMEM, SMEM, VMEM, VMEM, VMEM],
        out_specs=VMEM,
        compiler_params=pltpu.CompilerParams(vmem_limit_bytes=48 * 1024 * 1024),
        cost_estimate=pl.CostEstimate(
            flops=pairs * (2 * rows * tile + 10 * tile),
            transcendentals=pairs * 2 * tile,
            bytes_accessed=cd.size * 2 + sk.size * 8 + targets * rows * rank * 4,
        ),
    )(base, src.reshape(-1), counts, cd, sk, sw)


def far_tables(coef, skel, rank):
    cd = jnp.concatenate([coef, coef], axis=2)
    sk = skel.astype(jnp.float32)
    sw = jnp.concatenate([sk[:, rank:], sk[:, :rank]], axis=1)
    return cd, sk, sw


def body(
    values,
    points,
    basis,
    leaf_up,
    mid_up,
    box_up,
    leaf_skel,
    mid_skel,
    box_skel,
    top_skel,
    near_src,
    near_count,
    leaf_src,
    leaf_count,
    mid_src,
    mid_count,
    box_src,
    box_count,
    box_parent,
    top_src,
    top_count,
):
    leaves = values.shape[0]
    samples = values.shape[1]
    point_count = values.shape[2]
    rank_width = basis.shape[1]
    middle = leaves // 4
    box_nodes = leaves // 16
    top_nodes = top_count.shape[0]
    top_all = top_skel.shape[0]
    device = lax.axis_index("leaf")

    near_vals = padded(values, (("leaf", 0),), leaves)
    near_pts = padded(points, (("leaf", 0),), leaves).astype(jnp.float32).reshape(-1, point_count)
    near_rows = near_src - (device - 1) * leaves
    near_field = near_sum(
        jnp.full((1,), leaves, jnp.int32), near_rows, near_count, near_vals, near_pts
    )

    leaf_coef = jnp.einsum(
        "tsp,trp->tsr", values, basis, preferred_element_type=jnp.float32
    ).astype(jnp.bfloat16)
    mid_coef = (
        lift_up(leaf_coef, leaf_up, rank_width)
        .reshape(middle, 4, samples, rank_width)
        .sum(axis=1)
        .astype(jnp.bfloat16)
    )
    box_coef = (
        lift_up(mid_coef, mid_up, rank_width)
        .reshape(box_nodes, 4, samples, rank_width)
        .sum(axis=1)
        .astype(jnp.bfloat16)
    )
    box_term = lift_up(box_coef, box_up, rank_width).astype(jnp.bfloat16)
    group_term = (
        box_term.astype(jnp.float32)
        .reshape(box_nodes // 4, 4, samples * rank_width)
        .sum(axis=1)
        .astype(jnp.bfloat16)
    )
    all_groups = lax.all_gather(group_term, "leaf", axis=0, tiled=True)
    group_parent = box_parent.reshape(-1, 4)[:, 0]
    select = (
        group_parent[None, :] == jnp.arange(top_all, dtype=jnp.int32)[:, None]
    ).astype(jnp.bfloat16)
    top_coef = jnp.dot(select, all_groups, preferred_element_type=jnp.float32).astype(
        jnp.bfloat16
    )

    def pack(coef, skel):
        return jnp.concatenate([coef.reshape(coef.shape[0], -1), skel], axis=1)

    all_nodes = jnp.concatenate(
        [pack(leaf_coef, leaf_skel), pack(mid_coef, mid_skel), pack(box_coef, box_skel)], axis=0
    )
    per_device = leaves + middle + box_nodes
    node_table = padded(all_nodes, (("leaf", 0),), per_device).reshape(3, per_device, -1)
    coef_width = samples * rank_width

    def level(start, nodes, skel, src, counts):
        rows = node_table[:, start : start + nodes].reshape(3 * nodes, -1)
        coef = rows[:, :coef_width].reshape(3 * nodes, samples, rank_width)
        cd, sk, sw = far_tables(coef, rows[:, coef_width:], rank_width)
        local = src - (device - 1) * nodes
        return far_sum(jnp.full((1,), nodes, jnp.int32), local, counts, cd, sk, sw, rank_width)

    leaf_far = level(0, leaves, leaf_skel, leaf_src, leaf_count)
    mid_far = level(leaves, middle, mid_skel, mid_src, mid_count)
    box_far = level(leaves + middle, box_nodes, box_skel, box_src, box_count)

    top_cd, top_sk, top_sw = far_tables(
        top_coef.reshape(top_all, samples, rank_width), top_skel, rank_width
    )
    own_field = far_sum(
        (device * top_nodes).astype(jnp.int32).reshape(1),
        top_src,
        top_count,
        top_cd,
        top_sk,
        top_sw,
        rank_width,
    ).astype(jnp.bfloat16)
    top_field = lax.all_gather(
        own_field.reshape(top_nodes, samples * rank_width), "leaf", axis=0, tiled=True
    )
    own_parent = lax.dynamic_slice_in_dim(box_parent, device * box_nodes, box_nodes)
    parent_field = top_field[own_parent].reshape(box_nodes, samples, rank_width)
    box_field = (
        box_far
        + jnp.einsum(
            "bsr,bqr->bsq",
            parent_field,
            box_up.reshape(box_nodes, rank_width, rank_width),
            preferred_element_type=jnp.float32,
        )
    ).astype(jnp.bfloat16)
    mid_down = jnp.einsum(
        "bsr,bjqr->bjsq",
        box_field,
        mid_up.reshape(box_nodes, 4, rank_width, rank_width),
        preferred_element_type=jnp.float32,
    )
    mid_field = (mid_far + mid_down.reshape(middle, samples, rank_width)).astype(jnp.bfloat16)
    leaf_down = jnp.einsum(
        "bsr,bjqr->bjsq",
        mid_field,
        leaf_up.reshape(middle, 4, rank_width, rank_width),
        preferred_element_type=jnp.float32,
    )
    leaf_field = (leaf_far + leaf_down.reshape(leaves, samples, rank_width)).astype(jnp.bfloat16)
    return near_field + jnp.einsum(
        "tsr,trp->tsp", leaf_field, basis, preferred_element_type=jnp.float32
    )


def solution(mesh):
    return jax.shard_map(
        body,
        mesh=mesh,
        in_specs=(
            P("leaf", None, None),
            P("leaf", None, None),
            P("leaf", None, None),
            P("leaf", None),
            P("leaf", None),
            P("leaf", None),
            P("leaf", None),
            P("leaf", None),
            P("leaf", None),
            P(),
            P("leaf", None),
            P("leaf"),
            P("leaf", None),
            P("leaf"),
            P("leaf", None),
            P("leaf"),
            P("leaf", None),
            P("leaf"),
            P(),
            P("leaf", None),
            P("leaf"),
        ),
        out_specs=P("leaf", None, None),
        check_vma=False,
    )
```

```python
import functools

import jax
import jax.numpy as jnp
from jax import lax
from jax.experimental import pallas as pl
from jax.experimental.pallas import tpu as pltpu
from jax.sharding import PartitionSpec as P


def padded(shard, sides, width):
    for axis, dim in sides:
        size, length = (lax.axis_size(axis), shard.shape[dim])
        up = [(i, (i + 1) % size) for i in range(size - 1)]
        down = [(j, i) for i, j in up]
        last = lax.slice_in_dim(shard, length - width, length, axis=dim)
        leading = lax.slice_in_dim(shard, 0, width, axis=dim)
        before = lax.ppermute(last, axis, up)
        after = lax.ppermute(leading, axis, down)
        shard = jnp.concatenate([before, shard, after], axis=dim)
    return shard


def lift_up(coeffs, transfer, rank_width):
    nodes = coeffs.shape[0]
    matrices = transfer.reshape(nodes, rank_width, rank_width)
    return jnp.einsum("nsq,nqr->nsr", coeffs, matrices, preferred_element_type=jnp.float32)


NEG_LOG2E = -1.4426950408889634


def coupling(d2):
    return jnp.exp2((d2 * lax.rsqrt(d2)) * NEG_LOG2E).astype(jnp.bfloat16)


def near_kernel(base_ref, src_ref, cnt_ref, vals_ref, rows_ref, tgt_ref, out_ref, *, slots):
    targets = out_ref.shape[0]
    base = base_ref[0]

    def per_target(t, carry):
        frame = jnp.transpose(tgt_ref[t].astype(jnp.float32)).astype(jnp.bfloat16)

        def slot(j, acc):
            s = src_ref[t * slots + j]
            d2 = jnp.dot(frame, rows_ref[s], preferred_element_type=jnp.float32)
            k = coupling(d2)
            return acc + lax.dot_general(
                vals_ref[s], k, (((1,), (1,)), ((), ())), preferred_element_type=jnp.float32
            )

        acc = lax.fori_loop(0, cnt_ref[t], slot, jnp.zeros(out_ref.shape[1:], jnp.float32))
        out_ref[t] = 0.25 * acc
        return carry

    lax.fori_loop(0, targets, per_target, 0)


def far_kernel(base_ref, src_ref, cnt_ref, cd_ref, rows_ref, tgt_ref, out_ref, *, slots):
    targets, samples, rank = out_ref.shape
    width = cd_ref.shape[2]
    first_half = lax.broadcasted_iota(jnp.int32, (cd_ref.shape[1], width), 1) < rank
    zeros_c = jnp.zeros((cd_ref.shape[1], width), cd_ref.dtype)
    base = base_ref[0]

    def per_target(t, carry):
        frame = jnp.transpose(tgt_ref[base + t].astype(jnp.float32))[:rank].astype(jnp.bfloat16)
        count = cnt_ref[t]

        def slot(i, acc):
            j = 2 * i
            s1 = src_ref[t * slots + j]
            s2 = src_ref[t * slots + jnp.minimum(j + 1, slots - 1)]
            pair = jnp.where(first_half, rows_ref[s1], rows_ref[s2])
            d2 = jnp.dot(frame, pair, preferred_element_type=jnp.float32)
            k = coupling(d2)
            c2 = jnp.where(j + 1 < count, cd_ref[s2], zeros_c)
            cm = jnp.where(first_half, cd_ref[s1], c2)
            return acc + lax.dot_general(
                cm, k, (((1,), (1,)), ((), ())), preferred_element_type=jnp.float32
            )

        acc = lax.fori_loop(0, (count + 1) // 2, slot, jnp.zeros((samples, rank), jnp.float32))
        out_ref[t] = 0.25 * acc
        return carry

    lax.fori_loop(0, targets, per_target, 0)


SMEM = pl.BlockSpec(memory_space=pltpu.SMEM)
VMEM = pl.BlockSpec(memory_space=pltpu.VMEM)


def bf16_split(x):
    hi = lax.reduce_precision(x, exponent_bits=8, mantissa_bits=7)
    rest = x - hi
    mid = lax.reduce_precision(rest, exponent_bits=8, mantissa_bits=7)
    return [hi, mid, rest - mid]


def source_rows(frames):
    x, y = frames[:, 0], frames[:, 1]
    one = jnp.ones_like(x)
    parts = [-2.0 * x, -2.0 * y, one, one, one] + bf16_split(x * x + y * y)
    return jnp.stack(parts, axis=1).astype(jnp.bfloat16)


def target_rows(frames):
    x, y = frames[:, 0], frames[:, 1]
    one = jnp.ones_like(x)
    parts = [x, y] + bf16_split(x * x + y * y + 0.0025) + [one, one, one]
    return jnp.stack(parts, axis=1).astype(jnp.bfloat16)


def near_sum(base, src, counts, vals, rows, tgt):
    targets, slots = src.shape
    samples, width = vals.shape[1], vals.shape[2]
    tile = width * width
    pairs = targets * slots
    return pl.pallas_call(
        functools.partial(near_kernel, slots=slots),
        out_shape=jax.ShapeDtypeStruct((targets, samples, width), jnp.float32),
        in_specs=[SMEM, SMEM, SMEM, VMEM, VMEM, VMEM],
        out_specs=VMEM,
        compiler_params=pltpu.CompilerParams(vmem_limit_bytes=48 * 1024 * 1024),
        cost_estimate=pl.CostEstimate(
            flops=pairs * (2 * (samples + 8) * tile + 3 * tile),
            transcendentals=pairs * 2 * tile,
            bytes_accessed=vals.size * 2 + rows.size * 2 + targets * samples * width * 4,
        ),
    )(base, src.reshape(-1), counts, vals, rows, tgt)


def far_sum(base, src, counts, cd, rows, tgt, rank):
    targets, slots = src.shape
    samples, width = cd.shape[1], cd.shape[2]
    tile = rank * width
    pairs = targets * (slots + 1) // 2
    return pl.pallas_call(
        functools.partial(far_kernel, slots=slots),
        out_shape=jax.ShapeDtypeStruct((targets, samples, rank), jnp.float32),
        in_specs=[SMEM, SMEM, SMEM, VMEM, VMEM, VMEM],
        out_specs=VMEM,
        compiler_params=pltpu.CompilerParams(vmem_limit_bytes=48 * 1024 * 1024),
        cost_estimate=pl.CostEstimate(
            flops=pairs * (2 * (samples + 8) * tile + 3 * tile),
            transcendentals=pairs * 2 * tile,
            bytes_accessed=cd.size * 2 + rows.size * 4 + targets * samples * rank * 4,
        ),
    )(base, src.reshape(-1), counts, cd, rows, tgt)


def far_tables(coef, skel, rank):
    cd = jnp.concatenate([coef, coef], axis=2)
    frames = skel.astype(jnp.float32).reshape(skel.shape[0], 2, rank)
    rows = source_rows(frames)
    tgt = target_rows(frames)
    return cd, jnp.concatenate([rows, rows], axis=2), jnp.concatenate([tgt, tgt], axis=2)


def body(
    values,
    points,
    basis,
    leaf_up,
    mid_up,
    box_up,
    leaf_skel,
    mid_skel,
    box_skel,
    top_skel,
    near_src,
    near_count,
    leaf_src,
    leaf_count,
    mid_src,
    mid_count,
    box_src,
    box_count,
    box_parent,
    top_src,
    top_count,
):
    leaves = values.shape[0]
    samples = values.shape[1]
    point_count = values.shape[2]
    rank_width = basis.shape[1]
    middle = leaves // 4
    box_nodes = leaves // 16
    top_nodes = top_count.shape[0]
    top_all = top_skel.shape[0]
    device = lax.axis_index("leaf")

    near_vals = padded(values, (("leaf", 0),), leaves)
    near_pts = padded(points, (("leaf", 0),), leaves).astype(jnp.float32)
    near_rows = near_src - (device - 1) * leaves
    near_field = near_sum(
        jnp.full((1,), leaves, jnp.int32),
        near_rows,
        near_count,
        near_vals,
        source_rows(near_pts),
        target_rows(points.astype(jnp.float32)),
    )

    leaf_coef = jnp.einsum(
        "tsp,trp->tsr", values, basis, preferred_element_type=jnp.float32
    ).astype(jnp.bfloat16)
    mid_coef = (
        lift_up(leaf_coef, leaf_up, rank_width)
        .reshape(middle, 4, samples, rank_width)
        .sum(axis=1)
        .astype(jnp.bfloat16)
    )
    box_coef = (
        lift_up(mid_coef, mid_up, rank_width)
        .reshape(box_nodes, 4, samples, rank_width)
        .sum(axis=1)
        .astype(jnp.bfloat16)
    )
    box_term = lift_up(box_coef, box_up, rank_width).astype(jnp.bfloat16)
    group_term = (
        box_term.astype(jnp.float32)
        .reshape(box_nodes // 4, 4, samples * rank_width)
        .sum(axis=1)
        .astype(jnp.bfloat16)
    )
    all_groups = lax.all_gather(group_term, "leaf", axis=0, tiled=True)
    group_parent = box_parent.reshape(-1, 4)[:, 0]
    select = (
        group_parent[None, :] == jnp.arange(top_all, dtype=jnp.int32)[:, None]
    ).astype(jnp.bfloat16)
    top_coef = jnp.dot(select, all_groups, preferred_element_type=jnp.float32).astype(
        jnp.bfloat16
    )

    def pack(coef, skel):
        return jnp.concatenate([coef.reshape(coef.shape[0], -1), skel], axis=1)

    all_nodes = jnp.concatenate(
        [pack(leaf_coef, leaf_skel), pack(mid_coef, mid_skel), pack(box_coef, box_skel)], axis=0
    )
    per_device = leaves + middle + box_nodes
    node_table = padded(all_nodes, (("leaf", 0),), per_device).reshape(3, per_device, -1)
    coef_width = samples * rank_width

    def level(start, nodes, skel, src, counts):
        rows = node_table[:, start : start + nodes].reshape(3 * nodes, -1)
        coef = rows[:, :coef_width].reshape(3 * nodes, samples, rank_width)
        cd, rows_s, rows_t = far_tables(coef, rows[:, coef_width:], rank_width)
        local = src - (device - 1) * nodes
        return far_sum(jnp.full((1,), nodes, jnp.int32), local, counts, cd, rows_s, rows_t, rank_width)

    leaf_far = level(0, leaves, leaf_skel, leaf_src, leaf_count)
    mid_far = level(leaves, middle, mid_skel, mid_src, mid_count)
    box_far = level(leaves + middle, box_nodes, box_skel, box_src, box_count)

    top_cd, top_rows, top_tgt = far_tables(
        top_coef.reshape(top_all, samples, rank_width), top_skel, rank_width
    )
    own_field = far_sum(
        (device * top_nodes).astype(jnp.int32).reshape(1),
        top_src,
        top_count,
        top_cd,
        top_rows,
        top_tgt,
        rank_width,
    ).astype(jnp.bfloat16)
    top_field = lax.all_gather(
        own_field.reshape(top_nodes, samples * rank_width), "leaf", axis=0, tiled=True
    )
    own_parent = lax.dynamic_slice_in_dim(box_parent, device * box_nodes, box_nodes)
    parent_field = top_field[own_parent].reshape(box_nodes, samples, rank_width)
    box_field = (
        box_far
        + jnp.einsum(
            "bsr,bqr->bsq",
            parent_field,
            box_up.reshape(box_nodes, rank_width, rank_width),
            preferred_element_type=jnp.float32,
        )
    ).astype(jnp.bfloat16)
    mid_down = jnp.einsum(
        "bsr,bjqr->bjsq",
        box_field,
        mid_up.reshape(box_nodes, 4, rank_width, rank_width),
        preferred_element_type=jnp.float32,
    )
    mid_field = (mid_far + mid_down.reshape(middle, samples, rank_width)).astype(jnp.bfloat16)
    leaf_down = jnp.einsum(
        "bsr,bjqr->bjsq",
        mid_field,
        leaf_up.reshape(middle, 4, rank_width, rank_width),
        preferred_element_type=jnp.float32,
    )
    leaf_field = (leaf_far + leaf_down.reshape(leaves, samples, rank_width)).astype(jnp.bfloat16)
    return near_field + jnp.einsum(
        "tsr,trp->tsp", leaf_field, basis, preferred_element_type=jnp.float32
    )


def solution(mesh):
    return jax.shard_map(
        body,
        mesh=mesh,
        in_specs=(
            P("leaf", None, None),
            P("leaf", None, None),
            P("leaf", None, None),
            P("leaf", None),
            P("leaf", None),
            P("leaf", None),
            P("leaf", None),
            P("leaf", None),
            P("leaf", None),
            P(),
            P("leaf", None),
            P("leaf"),
            P("leaf", None),
            P("leaf"),
            P("leaf", None),
            P("leaf"),
            P("leaf", None),
            P("leaf"),
            P(),
            P("leaf", None),
            P("leaf"),
        ),
        out_specs=P("leaf", None, None),
        check_vma=False,
    )
```

```python
import functools

import jax
import jax.numpy as jnp
from jax import lax
from jax.experimental import pallas as pl
from jax.experimental.pallas import tpu as pltpu
from jax.sharding import PartitionSpec as P


def padded(shard, sides, width):
    for axis, dim in sides:
        size, length = (lax.axis_size(axis), shard.shape[dim])
        up = [(i, (i + 1) % size) for i in range(size - 1)]
        down = [(j, i) for i, j in up]
        last = lax.slice_in_dim(shard, length - width, length, axis=dim)
        leading = lax.slice_in_dim(shard, 0, width, axis=dim)
        before = lax.ppermute(last, axis, up)
        after = lax.ppermute(leading, axis, down)
        shard = jnp.concatenate([before, shard, after], axis=dim)
    return shard


def lift_up(coeffs, transfer, rank_width):
    nodes = coeffs.shape[0]
    matrices = transfer.reshape(nodes, rank_width, rank_width)
    return jnp.einsum("nsq,nqr->nsr", coeffs, matrices, preferred_element_type=jnp.float32)


NEG_LOG2E = -1.4426950408889634


def coupling(d2):
    return jnp.exp2((d2 * lax.rsqrt(d2)) * NEG_LOG2E).astype(jnp.bfloat16)


def nt_dot(a, b):
    return lax.dot_general(a, b, (((1,), (1,)), ((), ())), preferred_element_type=jnp.float32)


def near_kernel(base_ref, src_ref, cnt_ref, vals_ref, rows_ref, tgt_ref, out_ref, *, slots):
    targets = out_ref.shape[0]
    width = rows_ref.shape[2]

    def per_target(t, carry):
        frame = jnp.transpose(tgt_ref[t].astype(jnp.float32)).astype(jnp.bfloat16)

        def source(k):
            return src_ref[t * slots + jnp.minimum(k, slots - 1)]

        first = source(0)
        start = (
            jnp.zeros(out_ref.shape[1:], jnp.float32),
            jnp.zeros((width, width), jnp.bfloat16),
            first,
            jnp.dot(frame, rows_ref[first], preferred_element_type=jnp.float32),
        )

        def slot(j, state):
            acc, previous, held, d2 = state
            acc = acc + nt_dot(vals_ref[held], previous)
            following = jnp.dot(frame, rows_ref[source(j + 1)], preferred_element_type=jnp.float32)
            return acc, coupling(d2), source(j), following

        acc, last, held, _ = lax.fori_loop(0, cnt_ref[t], slot, start)
        out_ref[t] = 0.25 * (acc + nt_dot(vals_ref[held], last))
        return carry

    lax.fori_loop(0, targets, per_target, 0)


def far_kernel(base_ref, src_ref, cnt_ref, cd_ref, rows_ref, tgt_ref, out_ref, *, slots):
    targets, samples, rank = out_ref.shape
    width = cd_ref.shape[2]
    first_half = lax.broadcasted_iota(jnp.int32, (cd_ref.shape[1], width), 1) < rank
    zeros_c = jnp.zeros((cd_ref.shape[1], width), cd_ref.dtype)
    base = base_ref[0]

    def per_target(t, carry):
        frame = jnp.transpose(tgt_ref[base + t].astype(jnp.float32))[:rank].astype(jnp.bfloat16)
        count = cnt_ref[t]

        def source(k):
            return src_ref[t * slots + jnp.minimum(k, slots - 1)]

        def distances(i):
            pair = jnp.where(first_half, rows_ref[source(2 * i)], rows_ref[source(2 * i + 1)])
            return jnp.dot(frame, pair, preferred_element_type=jnp.float32)

        def coefficients(i):
            second = jnp.where(2 * i + 1 < count, cd_ref[source(2 * i + 1)], zeros_c)
            return jnp.where(first_half, cd_ref[source(2 * i)], second)

        start = (
            jnp.zeros((samples, rank), jnp.float32),
            jnp.zeros((rank, width), jnp.bfloat16),
            distances(0),
        )

        def slot(i, state):
            acc, previous, d2 = state
            acc = acc + nt_dot(coefficients(jnp.maximum(i - 1, 0)), previous)
            return acc, coupling(d2), distances(i + 1)

        steps = (count + 1) // 2
        acc, last, _ = lax.fori_loop(0, steps, slot, start)
        out_ref[t] = 0.25 * (acc + nt_dot(coefficients(steps - 1), last))
        return carry

    lax.fori_loop(0, targets, per_target, 0)


SMEM = pl.BlockSpec(memory_space=pltpu.SMEM)
VMEM = pl.BlockSpec(memory_space=pltpu.VMEM)


def bf16_split(x):
    hi = lax.reduce_precision(x, exponent_bits=8, mantissa_bits=7)
    rest = x - hi
    mid = lax.reduce_precision(rest, exponent_bits=8, mantissa_bits=7)
    return [hi, mid, rest - mid]


def source_rows(frames):
    x, y = frames[:, 0], frames[:, 1]
    one = jnp.ones_like(x)
    parts = [-2.0 * x, -2.0 * y, one, one, one] + bf16_split(x * x + y * y)
    return jnp.stack(parts, axis=1).astype(jnp.bfloat16)


def target_rows(frames):
    x, y = frames[:, 0], frames[:, 1]
    one = jnp.ones_like(x)
    parts = [x, y] + bf16_split(x * x + y * y + 0.0025) + [one, one, one]
    return jnp.stack(parts, axis=1).astype(jnp.bfloat16)


def near_sum(base, src, counts, vals, rows, tgt):
    targets, slots = src.shape
    samples, width = vals.shape[1], vals.shape[2]
    tile = width * width
    pairs = targets * slots
    return pl.pallas_call(
        functools.partial(near_kernel, slots=slots),
        out_shape=jax.ShapeDtypeStruct((targets, samples, width), jnp.float32),
        in_specs=[SMEM, SMEM, SMEM, VMEM, VMEM, VMEM],
        out_specs=VMEM,
        compiler_params=pltpu.CompilerParams(vmem_limit_bytes=48 * 1024 * 1024),
        cost_estimate=pl.CostEstimate(
            flops=pairs * (2 * (samples + 8) * tile + 3 * tile),
            transcendentals=pairs * 2 * tile,
            bytes_accessed=vals.size * 2 + rows.size * 2 + targets * samples * width * 4,
        ),
    )(base, src.reshape(-1), counts, vals, rows, tgt)


def far_sum(base, src, counts, cd, rows, tgt, rank):
    targets, slots = src.shape
    samples, width = cd.shape[1], cd.shape[2]
    tile = rank * width
    pairs = targets * (slots + 1) // 2
    return pl.pallas_call(
        functools.partial(far_kernel, slots=slots),
        out_shape=jax.ShapeDtypeStruct((targets, samples, rank), jnp.float32),
        in_specs=[SMEM, SMEM, SMEM, VMEM, VMEM, VMEM],
        out_specs=VMEM,
        compiler_params=pltpu.CompilerParams(vmem_limit_bytes=48 * 1024 * 1024),
        cost_estimate=pl.CostEstimate(
            flops=pairs * (2 * (samples + 8) * tile + 3 * tile),
            transcendentals=pairs * 2 * tile,
            bytes_accessed=cd.size * 2 + rows.size * 4 + targets * samples * rank * 4,
        ),
    )(base, src.reshape(-1), counts, cd, rows, tgt)


def far_tables(coef, skel, rank):
    cd = jnp.concatenate([coef, coef], axis=2)
    frames = skel.astype(jnp.float32).reshape(skel.shape[0], 2, rank)
    rows = source_rows(frames)
    tgt = target_rows(frames)
    return cd, jnp.concatenate([rows, rows], axis=2), jnp.concatenate([tgt, tgt], axis=2)


def body(
    values,
    points,
    basis,
    leaf_up,
    mid_up,
    box_up,
    leaf_skel,
    mid_skel,
    box_skel,
    top_skel,
    near_src,
    near_count,
    leaf_src,
    leaf_count,
    mid_src,
    mid_count,
    box_src,
    box_count,
    box_parent,
    top_src,
    top_count,
):
    leaves = values.shape[0]
    samples = values.shape[1]
    point_count = values.shape[2]
    rank_width = basis.shape[1]
    middle = leaves // 4
    box_nodes = leaves // 16
    top_nodes = top_count.shape[0]
    top_all = top_skel.shape[0]
    device = lax.axis_index("leaf")

    near_vals = padded(values, (("leaf", 0),), leaves)
    near_pts = padded(points, (("leaf", 0),), leaves).astype(jnp.float32)
    near_rows = near_src - (device - 1) * leaves
    near_field = near_sum(
        jnp.full((1,), leaves, jnp.int32),
        near_rows,
        near_count,
        near_vals,
        source_rows(near_pts),
        target_rows(points.astype(jnp.float32)),
    )

    leaf_coef = jnp.einsum(
        "tsp,trp->tsr", values, basis, preferred_element_type=jnp.float32
    ).astype(jnp.bfloat16)
    mid_coef = (
        lift_up(leaf_coef, leaf_up, rank_width)
        .reshape(middle, 4, samples, rank_width)
        .sum(axis=1)
        .astype(jnp.bfloat16)
    )
    box_coef = (
        lift_up(mid_coef, mid_up, rank_width)
        .reshape(box_nodes, 4, samples, rank_width)
        .sum(axis=1)
        .astype(jnp.bfloat16)
    )
    box_term = lift_up(box_coef, box_up, rank_width).astype(jnp.bfloat16)
    group_term = (
        box_term.astype(jnp.float32)
        .reshape(box_nodes // 4, 4, samples * rank_width)
        .sum(axis=1)
        .astype(jnp.bfloat16)
    )
    all_groups = lax.all_gather(group_term, "leaf", axis=0, tiled=True)
    group_parent = box_parent.reshape(-1, 4)[:, 0]
    select = (
        group_parent[None, :] == jnp.arange(top_all, dtype=jnp.int32)[:, None]
    ).astype(jnp.bfloat16)
    top_coef = jnp.dot(select, all_groups, preferred_element_type=jnp.float32).astype(
        jnp.bfloat16
    )

    def pack(coef, skel):
        return jnp.concatenate([coef.reshape(coef.shape[0], -1), skel], axis=1)

    all_nodes = jnp.concatenate(
        [pack(leaf_coef, leaf_skel), pack(mid_coef, mid_skel), pack(box_coef, box_skel)], axis=0
    )
    per_device = leaves + middle + box_nodes
    node_table = padded(all_nodes, (("leaf", 0),), per_device).reshape(3, per_device, -1)
    coef_width = samples * rank_width

    def level(start, nodes, skel, src, counts):
        rows = node_table[:, start : start + nodes].reshape(3 * nodes, -1)
        coef = rows[:, :coef_width].reshape(3 * nodes, samples, rank_width)
        cd, rows_s, rows_t = far_tables(coef, rows[:, coef_width:], rank_width)
        local = src - (device - 1) * nodes
        return far_sum(jnp.full((1,), nodes, jnp.int32), local, counts, cd, rows_s, rows_t, rank_width)

    leaf_far = level(0, leaves, leaf_skel, leaf_src, leaf_count)
    mid_far = level(leaves, middle, mid_skel, mid_src, mid_count)
    box_far = level(leaves + middle, box_nodes, box_skel, box_src, box_count)

    top_cd, top_rows, top_tgt = far_tables(
        top_coef.reshape(top_all, samples, rank_width), top_skel, rank_width
    )
    own_field = far_sum(
        (device * top_nodes).astype(jnp.int32).reshape(1),
        top_src,
        top_count,
        top_cd,
        top_rows,
        top_tgt,
        rank_width,
    ).astype(jnp.bfloat16)
    top_field = lax.all_gather(
        own_field.reshape(top_nodes, samples * rank_width), "leaf", axis=0, tiled=True
    )
    own_parent = lax.dynamic_slice_in_dim(box_parent, device * box_nodes, box_nodes)
    parent_field = top_field[own_parent].reshape(box_nodes, samples, rank_width)
    box_field = (
        box_far
        + jnp.einsum(
            "bsr,bqr->bsq",
            parent_field,
            box_up.reshape(box_nodes, rank_width, rank_width),
            preferred_element_type=jnp.float32,
        )
    ).astype(jnp.bfloat16)
    mid_down = jnp.einsum(
        "bsr,bjqr->bjsq",
        box_field,
        mid_up.reshape(box_nodes, 4, rank_width, rank_width),
        preferred_element_type=jnp.float32,
    )
    mid_field = (mid_far + mid_down.reshape(middle, samples, rank_width)).astype(jnp.bfloat16)
    leaf_down = jnp.einsum(
        "bsr,bjqr->bjsq",
        mid_field,
        leaf_up.reshape(middle, 4, rank_width, rank_width),
        preferred_element_type=jnp.float32,
    )
    leaf_field = (leaf_far + leaf_down.reshape(leaves, samples, rank_width)).astype(jnp.bfloat16)
    return near_field + jnp.einsum(
        "tsr,trp->tsp", leaf_field, basis, preferred_element_type=jnp.float32
    )


def solution(mesh):
    return jax.shard_map(
        body,
        mesh=mesh,
        in_specs=(
            P("leaf", None, None),
            P("leaf", None, None),
            P("leaf", None, None),
            P("leaf", None),
            P("leaf", None),
            P("leaf", None),
            P("leaf", None),
            P("leaf", None),
            P("leaf", None),
            P(),
            P("leaf", None),
            P("leaf"),
            P("leaf", None),
            P("leaf"),
            P("leaf", None),
            P("leaf"),
            P("leaf", None),
            P("leaf"),
            P(),
            P("leaf", None),
            P("leaf"),
        ),
        out_specs=P("leaf", None, None),
        check_vma=False,
    )
```

```python
import functools

import jax
import jax.numpy as jnp
from jax import lax
from jax.experimental import pallas as pl
from jax.experimental.pallas import tpu as pltpu
from jax.sharding import PartitionSpec as P


def padded(shard, sides, width):
    for axis, dim in sides:
        size, length = (lax.axis_size(axis), shard.shape[dim])
        up = [(i, (i + 1) % size) for i in range(size - 1)]
        down = [(j, i) for i, j in up]
        last = lax.slice_in_dim(shard, length - width, length, axis=dim)
        leading = lax.slice_in_dim(shard, 0, width, axis=dim)
        before = lax.ppermute(last, axis, up)
        after = lax.ppermute(leading, axis, down)
        shard = jnp.concatenate([before, shard, after], axis=dim)
    return shard


def gather_rows(block, axis):
    size = lax.axis_size(axis)
    rows = block.shape[0]
    full = jnp.zeros((rows * size,) + block.shape[1:], block.dtype)
    full = lax.dynamic_update_slice_in_dim(full, block, lax.axis_index(axis) * rows, axis=0)
    return lax.psum(full, axis)


def lift_up(coeffs, transfer, rank_width):
    nodes = coeffs.shape[0]
    matrices = transfer.reshape(nodes, rank_width, rank_width)
    return jnp.einsum("nsq,nqr->nsr", coeffs, matrices, preferred_element_type=jnp.float32)


NEG_LOG2E = -1.4426950408889634


def coupling(d2):
    return jnp.exp2((d2 * lax.rsqrt(d2)) * NEG_LOG2E).astype(jnp.bfloat16)


def nt_dot(a, b):
    return lax.dot_general(a, b, (((1,), (1,)), ((), ())), preferred_element_type=jnp.float32)


NEAR_UNROLL = 5
FAR_UNROLL = 4


def near_kernel(base_ref, src_ref, cnt_ref, vals_ref, rows_ref, tgt_ref, out_ref, *, slots):
    targets = out_ref.shape[0]
    zeros_v = jnp.zeros(vals_ref.shape[1:], vals_ref.dtype)

    def per_target(t, carry):
        frame = jnp.transpose(tgt_ref[t].astype(jnp.float32)).astype(jnp.bfloat16)
        count = cnt_ref[t]

        def step(i, acc):
            for u in range(NEAR_UNROLL):
                k = NEAR_UNROLL * i + u
                s = src_ref[t * slots + jnp.minimum(k, slots - 1)]
                d2 = jnp.dot(frame, rows_ref[s], preferred_element_type=jnp.float32)
                v = jnp.where(k < count, vals_ref[s], zeros_v)
                acc = acc + nt_dot(v, coupling(d2))
            return acc

        steps = (count + NEAR_UNROLL - 1) // NEAR_UNROLL
        acc = lax.fori_loop(0, steps, step, jnp.zeros(out_ref.shape[1:], jnp.float32))
        out_ref[t] = 0.25 * acc
        return carry

    lax.fori_loop(0, targets, per_target, 0)


def far_kernel(base_ref, src_ref, cnt_ref, cd_ref, rows_ref, tgt_ref, out_ref, *, slots):
    targets, samples, rank = out_ref.shape
    width = cd_ref.shape[2]
    first_half = lax.broadcasted_iota(jnp.int32, (cd_ref.shape[1], width), 1) < rank
    zeros_c = jnp.zeros((cd_ref.shape[1], width), cd_ref.dtype)
    base = base_ref[0]

    def per_target(t, carry):
        frame = jnp.transpose(tgt_ref[base + t].astype(jnp.float32))[:rank].astype(jnp.bfloat16)
        count = cnt_ref[t]

        def source(k):
            return src_ref[t * slots + jnp.minimum(k, slots - 1)]

        def step(i, acc):
            for u in range(FAR_UNROLL):
                a = 2 * (FAR_UNROLL * i + u)
                sa, sb = source(a), source(a + 1)
                pair = jnp.where(first_half, rows_ref[sa], rows_ref[sb])
                d2 = jnp.dot(frame, pair, preferred_element_type=jnp.float32)
                ca = jnp.where(a < count, cd_ref[sa], zeros_c)
                cb = jnp.where(a + 1 < count, cd_ref[sb], zeros_c)
                acc = acc + nt_dot(jnp.where(first_half, ca, cb), coupling(d2))
            return acc

        steps = (count + 2 * FAR_UNROLL - 1) // (2 * FAR_UNROLL)
        acc = lax.fori_loop(0, steps, step, jnp.zeros((samples, rank), jnp.float32))
        out_ref[t] = 0.25 * acc
        return carry

    lax.fori_loop(0, targets, per_target, 0)


SMEM = pl.BlockSpec(memory_space=pltpu.SMEM)
VMEM = pl.BlockSpec(memory_space=pltpu.VMEM)


def bf16_split(x):
    hi = lax.reduce_precision(x, exponent_bits=8, mantissa_bits=7)
    rest = x - hi
    mid = lax.reduce_precision(rest, exponent_bits=8, mantissa_bits=7)
    return [hi, mid, rest - mid]


def source_rows(frames):
    x, y = frames[:, 0], frames[:, 1]
    one = jnp.ones_like(x)
    parts = [-2.0 * x, -2.0 * y, one, one, one] + bf16_split(x * x + y * y)
    return jnp.stack(parts, axis=1).astype(jnp.bfloat16)


def target_rows(frames):
    x, y = frames[:, 0], frames[:, 1]
    one = jnp.ones_like(x)
    parts = [x, y] + bf16_split(x * x + y * y + 0.0025) + [one, one, one]
    return jnp.stack(parts, axis=1).astype(jnp.bfloat16)


def near_sum(base, src, counts, vals, rows, tgt):
    targets, slots = src.shape
    samples, width = vals.shape[1], vals.shape[2]
    tile = width * width
    pairs = targets * slots
    return pl.pallas_call(
        functools.partial(near_kernel, slots=slots),
        out_shape=jax.ShapeDtypeStruct((targets, samples, width), jnp.float32),
        in_specs=[SMEM, SMEM, SMEM, VMEM, VMEM, VMEM],
        out_specs=VMEM,
        compiler_params=pltpu.CompilerParams(vmem_limit_bytes=48 * 1024 * 1024),
        cost_estimate=pl.CostEstimate(
            flops=pairs * (2 * (samples + 8) * tile + 3 * tile),
            transcendentals=pairs * 2 * tile,
            bytes_accessed=vals.size * 2 + rows.size * 2 + targets * samples * width * 4,
        ),
    )(base, src.reshape(-1), counts, vals, rows, tgt)


def far_sum(base, src, counts, cd, rows, tgt, rank):
    targets, slots = src.shape
    samples, width = cd.shape[1], cd.shape[2]
    tile = rank * width
    pairs = targets * (slots + 1) // 2
    return pl.pallas_call(
        functools.partial(far_kernel, slots=slots),
        out_shape=jax.ShapeDtypeStruct((targets, samples, rank), jnp.float32),
        in_specs=[SMEM, SMEM, SMEM, VMEM, VMEM, VMEM],
        out_specs=VMEM,
        compiler_params=pltpu.CompilerParams(vmem_limit_bytes=48 * 1024 * 1024),
        cost_estimate=pl.CostEstimate(
            flops=pairs * (2 * (samples + 8) * tile + 3 * tile),
            transcendentals=pairs * 2 * tile,
            bytes_accessed=cd.size * 2 + rows.size * 4 + targets * samples * rank * 4,
        ),
    )(base, src.reshape(-1), counts, cd, rows, tgt)


def far_tables(coef, skel, rank):
    cd = jnp.concatenate([coef, coef], axis=2)
    frames = skel.astype(jnp.float32).reshape(skel.shape[0], 2, rank)
    rows = source_rows(frames)
    tgt = target_rows(frames)
    return cd, jnp.concatenate([rows, rows], axis=2), jnp.concatenate([tgt, tgt], axis=2)


def body(
    values,
    points,
    basis,
    leaf_up,
    mid_up,
    box_up,
    leaf_skel,
    mid_skel,
    box_skel,
    top_skel,
    near_src,
    near_count,
    leaf_src,
    leaf_count,
    mid_src,
    mid_count,
    box_src,
    box_count,
    box_parent,
    top_src,
    top_count,
):
    leaves = values.shape[0]
    samples = values.shape[1]
    point_count = values.shape[2]
    rank_width = basis.shape[1]
    middle = leaves // 4
    box_nodes = leaves // 16
    top_nodes = top_count.shape[0]
    top_all = top_skel.shape[0]
    device = lax.axis_index("leaf")

    near_vals = padded(values, (("leaf", 0),), leaves)
    near_pts = padded(points, (("leaf", 0),), leaves).astype(jnp.float32)
    near_rows = near_src - (device - 1) * leaves
    near_field = near_sum(
        jnp.full((1,), leaves, jnp.int32),
        near_rows,
        near_count,
        near_vals,
        source_rows(near_pts),
        target_rows(points.astype(jnp.float32)),
    )

    leaf_coef = jnp.einsum(
        "tsp,trp->tsr", values, basis, preferred_element_type=jnp.float32
    ).astype(jnp.bfloat16)
    mid_coef = (
        lift_up(leaf_coef, leaf_up, rank_width)
        .reshape(middle, 4, samples, rank_width)
        .sum(axis=1)
        .astype(jnp.bfloat16)
    )
    box_coef = (
        lift_up(mid_coef, mid_up, rank_width)
        .reshape(box_nodes, 4, samples, rank_width)
        .sum(axis=1)
        .astype(jnp.bfloat16)
    )
    box_term = lift_up(box_coef, box_up, rank_width).astype(jnp.bfloat16)
    group_term = (
        box_term.astype(jnp.float32)
        .reshape(box_nodes // 4, 4, samples * rank_width)
        .sum(axis=1)
        .astype(jnp.bfloat16)
    )
    all_groups = gather_rows(group_term, "leaf")
    group_parent = box_parent.reshape(-1, 4)[:, 0]
    select = (
        group_parent[None, :] == jnp.arange(top_all, dtype=jnp.int32)[:, None]
    ).astype(jnp.bfloat16)
    top_coef = jnp.dot(select, all_groups, preferred_element_type=jnp.float32).astype(
        jnp.bfloat16
    )

    def pack(coef, skel):
        return jnp.concatenate([coef.reshape(coef.shape[0], -1), skel], axis=1)

    all_nodes = jnp.concatenate(
        [pack(leaf_coef, leaf_skel), pack(mid_coef, mid_skel), pack(box_coef, box_skel)], axis=0
    )
    per_device = leaves + middle + box_nodes
    node_table = padded(all_nodes, (("leaf", 0),), per_device).reshape(3, per_device, -1)
    coef_width = samples * rank_width

    def level(start, nodes, skel, src, counts):
        rows = node_table[:, start : start + nodes].reshape(3 * nodes, -1)
        coef = rows[:, :coef_width].reshape(3 * nodes, samples, rank_width)
        cd, rows_s, rows_t = far_tables(coef, rows[:, coef_width:], rank_width)
        local = src - (device - 1) * nodes
        return far_sum(jnp.full((1,), nodes, jnp.int32), local, counts, cd, rows_s, rows_t, rank_width)

    leaf_far = level(0, leaves, leaf_skel, leaf_src, leaf_count)
    mid_far = level(leaves, middle, mid_skel, mid_src, mid_count)
    box_far = level(leaves + middle, box_nodes, box_skel, box_src, box_count)

    top_cd, top_rows, top_tgt = far_tables(
        top_coef.reshape(top_all, samples, rank_width), top_skel, rank_width
    )
    own_field = far_sum(
        (device * top_nodes).astype(jnp.int32).reshape(1),
        top_src,
        top_count,
        top_cd,
        top_rows,
        top_tgt,
        rank_width,
    ).astype(jnp.bfloat16)
    top_field = gather_rows(own_field.reshape(top_nodes, samples * rank_width), "leaf")
    own_parent = lax.dynamic_slice_in_dim(box_parent, device * box_nodes, box_nodes)
    parent_field = top_field[own_parent].reshape(box_nodes, samples, rank_width)
    box_field = (
        box_far
        + jnp.einsum(
            "bsr,bqr->bsq",
            parent_field,
            box_up.reshape(box_nodes, rank_width, rank_width),
            preferred_element_type=jnp.float32,
        )
    ).astype(jnp.bfloat16)
    mid_down = jnp.einsum(
        "bsr,bjqr->bjsq",
        box_field,
        mid_up.reshape(box_nodes, 4, rank_width, rank_width),
        preferred_element_type=jnp.float32,
    )
    mid_field = (mid_far + mid_down.reshape(middle, samples, rank_width)).astype(jnp.bfloat16)
    leaf_down = jnp.einsum(
        "bsr,bjqr->bjsq",
        mid_field,
        leaf_up.reshape(middle, 4, rank_width, rank_width),
        preferred_element_type=jnp.float32,
    )
    leaf_field = (leaf_far + leaf_down.reshape(leaves, samples, rank_width)).astype(jnp.bfloat16)
    return near_field + jnp.einsum(
        "tsr,trp->tsp", leaf_field, basis, preferred_element_type=jnp.float32
    )


def solution(mesh):
    return jax.shard_map(
        body,
        mesh=mesh,
        in_specs=(
            P("leaf", None, None),
            P("leaf", None, None),
            P("leaf", None, None),
            P("leaf", None),
            P("leaf", None),
            P("leaf", None),
            P("leaf", None),
            P("leaf", None),
            P("leaf", None),
            P(),
            P("leaf", None),
            P("leaf"),
            P("leaf", None),
            P("leaf"),
            P("leaf", None),
            P("leaf"),
            P("leaf", None),
            P("leaf"),
            P(),
            P("leaf", None),
            P("leaf"),
        ),
        out_specs=P("leaf", None, None),
        check_vma=False,
    )
```

```python
import functools

import jax
import jax.numpy as jnp
from jax import lax
from jax.experimental import pallas as pl
from jax.experimental.pallas import tpu as pltpu
from jax.sharding import PartitionSpec as P


def padded(shard, sides, width):
    for axis, dim in sides:
        size, length = (lax.axis_size(axis), shard.shape[dim])
        up = [(i, (i + 1) % size) for i in range(size - 1)]
        down = [(j, i) for i, j in up]
        last = lax.slice_in_dim(shard, length - width, length, axis=dim)
        leading = lax.slice_in_dim(shard, 0, width, axis=dim)
        before = lax.ppermute(last, axis, up)
        after = lax.ppermute(leading, axis, down)
        shard = jnp.concatenate([before, shard, after], axis=dim)
    return shard


def gather_rows(block, axis):
    size = lax.axis_size(axis)
    rows = block.shape[0]
    full = jnp.zeros((rows * size,) + block.shape[1:], block.dtype)
    full = lax.dynamic_update_slice_in_dim(full, block, lax.axis_index(axis) * rows, axis=0)
    return lax.psum(full, axis)


def lift_up(coeffs, transfer, rank_width):
    nodes = coeffs.shape[0]
    matrices = transfer.reshape(nodes, rank_width, rank_width)
    return jnp.einsum("nsq,nqr->nsr", coeffs, matrices, preferred_element_type=jnp.float32)


NEG_LOG2E = -1.4426950408889634


def coupling(d2):
    return jnp.exp2((d2 * lax.rsqrt(d2)) * NEG_LOG2E).astype(jnp.bfloat16)


def nt_dot(a, b):
    return lax.dot_general(a, b, (((1,), (1,)), ((), ())), preferred_element_type=jnp.float32)


NEAR_UNROLL = 5
FAR_UNROLL = 4


def near_kernel(base_ref, src_ref, cnt_ref, vals_ref, rows_ref, tgt_ref, out_ref, *, slots):
    targets = out_ref.shape[0]
    zeros_v = jnp.zeros(vals_ref.shape[1:], vals_ref.dtype)

    def per_target(t, carry):
        frame = jnp.transpose(tgt_ref[t].astype(jnp.float32)).astype(jnp.bfloat16)
        count = cnt_ref[t]

        def step(i, acc):
            for u in range(NEAR_UNROLL):
                k = NEAR_UNROLL * i + u
                s = src_ref[t * slots + jnp.minimum(k, slots - 1)]
                d2 = jnp.dot(frame, rows_ref[s], preferred_element_type=jnp.float32)
                v = jnp.where(k < count, vals_ref[s], zeros_v)
                acc = acc + nt_dot(v, coupling(d2))
            return acc

        steps = (count + NEAR_UNROLL - 1) // NEAR_UNROLL
        acc = lax.fori_loop(0, steps, step, jnp.zeros(out_ref.shape[1:], jnp.float32))
        out_ref[t] = 0.25 * acc
        return carry

    lax.fori_loop(0, targets, per_target, 0)


def far_kernel(base_ref, src_ref, cnt_ref, cd_ref, rows_ref, tgt_ref, out_ref, *, slots):
    targets, samples, rank = out_ref.shape
    width = cd_ref.shape[2]
    first_half = lax.broadcasted_iota(jnp.int32, (cd_ref.shape[1], width), 1) < rank
    zeros_c = jnp.zeros((cd_ref.shape[1], width), cd_ref.dtype)
    base = base_ref[0]

    def per_target(t, carry):
        frame = jnp.transpose(tgt_ref[base + t].astype(jnp.float32))[:rank].astype(jnp.bfloat16)
        count = cnt_ref[t]

        def source(k):
            return src_ref[t * slots + jnp.minimum(k, slots - 1)]

        def step(i, acc):
            for u in range(FAR_UNROLL):
                a = 2 * (FAR_UNROLL * i + u)
                sa, sb = source(a), source(a + 1)
                pair = jnp.where(first_half, rows_ref[sa], rows_ref[sb])
                d2 = jnp.dot(frame, pair, preferred_element_type=jnp.float32)
                ca = jnp.where(a < count, cd_ref[sa], zeros_c)
                cb = jnp.where(a + 1 < count, cd_ref[sb], zeros_c)
                acc = acc + nt_dot(jnp.where(first_half, ca, cb), coupling(d2))
            return acc

        steps = (count + 2 * FAR_UNROLL - 1) // (2 * FAR_UNROLL)
        acc = lax.fori_loop(0, steps, step, jnp.zeros((samples, rank), jnp.float32))
        out_ref[t] = 0.25 * acc
        return carry

    lax.fori_loop(0, targets, per_target, 0)


SMEM = pl.BlockSpec(memory_space=pltpu.SMEM)
VMEM = pl.BlockSpec(memory_space=pltpu.VMEM)


def bf16_split(x):
    hi = lax.reduce_precision(x, exponent_bits=8, mantissa_bits=7)
    rest = x - hi
    mid = lax.reduce_precision(rest, exponent_bits=8, mantissa_bits=7)
    return [hi, mid, rest - mid]


def source_rows(frames):
    x, y = frames[:, 0], frames[:, 1]
    one = jnp.ones_like(x)
    parts = [-2.0 * x, -2.0 * y, one, one, one] + bf16_split(x * x + y * y)
    return jnp.stack(parts, axis=1).astype(jnp.bfloat16)


def target_rows(frames):
    x, y = frames[:, 0], frames[:, 1]
    one = jnp.ones_like(x)
    parts = [x, y] + bf16_split(x * x + y * y + 0.0025) + [one, one, one]
    return jnp.stack(parts, axis=1).astype(jnp.bfloat16)


def near_sum(base, src, counts, vals, rows, tgt):
    targets, slots = src.shape
    samples, width = vals.shape[1], vals.shape[2]
    tile = width * width
    pairs = targets * slots
    return pl.pallas_call(
        functools.partial(near_kernel, slots=slots),
        out_shape=jax.ShapeDtypeStruct((targets, samples, width), jnp.float32),
        in_specs=[SMEM, SMEM, SMEM, VMEM, VMEM, VMEM],
        out_specs=VMEM,
        compiler_params=pltpu.CompilerParams(vmem_limit_bytes=48 * 1024 * 1024),
        cost_estimate=pl.CostEstimate(
            flops=pairs * (2 * (samples + 8) * tile + 3 * tile),
            transcendentals=pairs * 2 * tile,
            bytes_accessed=vals.size * 2 + rows.size * 2 + targets * samples * width * 4,
        ),
    )(base, src.reshape(-1), counts, vals, rows, tgt)


def far_sum(base, src, counts, cd, rows, tgt, rank):
    targets, slots = src.shape
    samples, width = cd.shape[1], cd.shape[2]
    tile = rank * width
    pairs = targets * (slots + 1) // 2
    return pl.pallas_call(
        functools.partial(far_kernel, slots=slots),
        out_shape=jax.ShapeDtypeStruct((targets, samples, rank), jnp.float32),
        in_specs=[SMEM, SMEM, SMEM, VMEM, VMEM, VMEM],
        out_specs=VMEM,
        compiler_params=pltpu.CompilerParams(vmem_limit_bytes=48 * 1024 * 1024),
        cost_estimate=pl.CostEstimate(
            flops=pairs * (2 * (samples + 8) * tile + 3 * tile),
            transcendentals=pairs * 2 * tile,
            bytes_accessed=cd.size * 2 + rows.size * 4 + targets * samples * rank * 4,
        ),
    )(base, src.reshape(-1), counts, cd, rows, tgt)


def far_tables(coef, skel, rank):
    cd = jnp.concatenate([coef, coef], axis=2)
    frames = skel.astype(jnp.float32).reshape(skel.shape[0], 2, rank)
    rows = source_rows(frames)
    tgt = target_rows(frames)
    return cd, jnp.concatenate([rows, rows], axis=2), jnp.concatenate([tgt, tgt], axis=2)


def body(
    values,
    points,
    basis,
    leaf_up,
    mid_up,
    box_up,
    leaf_skel,
    mid_skel,
    box_skel,
    top_skel,
    near_src,
    near_count,
    leaf_src,
    leaf_count,
    mid_src,
    mid_count,
    box_src,
    box_count,
    box_parent,
    top_src,
    top_count,
):
    leaves = values.shape[0]
    samples = values.shape[1]
    rank_width = basis.shape[1]
    middle = leaves // 4
    box_nodes = leaves // 16
    top_nodes = top_count.shape[0]
    top_all = top_skel.shape[0]
    device = lax.axis_index("leaf")

    near_vals = padded(values, (("leaf", 0),), leaves)
    near_pts = padded(points, (("leaf", 0),), leaves).astype(jnp.float32)
    near_rows = near_src - (device - 1) * leaves
    near_field = near_sum(
        jnp.full((1,), leaves, jnp.int32),
        near_rows,
        near_count,
        near_vals,
        source_rows(near_pts),
        target_rows(points.astype(jnp.float32)),
    )

    leaf_coef = jnp.einsum(
        "tsp,trp->tsr", values, basis, preferred_element_type=jnp.float32
    ).astype(jnp.bfloat16)
    mid_coef = (
        lift_up(leaf_coef, leaf_up, rank_width)
        .reshape(middle, 4, samples, rank_width)
        .sum(axis=1)
        .astype(jnp.bfloat16)
    )
    box_coef = (
        lift_up(mid_coef, mid_up, rank_width)
        .reshape(box_nodes, 4, samples, rank_width)
        .sum(axis=1)
        .astype(jnp.bfloat16)
    )
    box_term = lift_up(box_coef, box_up, rank_width).astype(jnp.bfloat16)
    group_term = (
        box_term.astype(jnp.float32)
        .reshape(box_nodes // 4, 4, samples * rank_width)
        .sum(axis=1)
        .astype(jnp.bfloat16)
    )
    all_groups = gather_rows(group_term, "leaf")
    group_parent = box_parent.reshape(-1, 4)[:, 0]
    select = (
        group_parent[None, :] == jnp.arange(top_all, dtype=jnp.int32)[:, None]
    ).astype(jnp.bfloat16)
    top_coef = jnp.dot(select, all_groups, preferred_element_type=jnp.float32).astype(
        jnp.bfloat16
    )

    def pack(coef, skel):
        return jnp.concatenate([coef.reshape(coef.shape[0], -1), skel], axis=1)

    all_nodes = jnp.concatenate(
        [pack(leaf_coef, leaf_skel), pack(mid_coef, mid_skel), pack(box_coef, box_skel)], axis=0
    )
    per_device = leaves + middle + box_nodes
    node_table = padded(all_nodes, (("leaf", 0),), per_device).reshape(3, per_device, -1)
    coef_width = samples * rank_width

    def level(start, nodes, src, counts):
        rows = node_table[:, start : start + nodes].reshape(3 * nodes, -1)
        coef = rows[:, :coef_width].reshape(3 * nodes, samples, rank_width)
        cd, rows_s, rows_t = far_tables(coef, rows[:, coef_width:], rank_width)
        local = src - (device - 1) * nodes
        return far_sum(jnp.full((1,), nodes, jnp.int32), local, counts, cd, rows_s, rows_t, rank_width)

    leaf_far = level(0, leaves, leaf_src, leaf_count)
    mid_far = level(leaves, middle, mid_src, mid_count)
    box_far = level(leaves + middle, box_nodes, box_src, box_count)

    top_cd, top_rows, top_tgt = far_tables(
        top_coef.reshape(top_all, samples, rank_width), top_skel, rank_width
    )
    own_field = far_sum(
        (device * top_nodes).astype(jnp.int32).reshape(1),
        top_src,
        top_count,
        top_cd,
        top_rows,
        top_tgt,
        rank_width,
    ).astype(jnp.bfloat16)
    top_field = gather_rows(own_field.reshape(top_nodes, samples * rank_width), "leaf")
    own_parent = lax.dynamic_slice_in_dim(box_parent, device * box_nodes, box_nodes)
    parent_field = top_field[own_parent].reshape(box_nodes, samples, rank_width)
    box_field = (
        box_far
        + jnp.einsum(
            "bsr,bqr->bsq",
            parent_field,
            box_up.reshape(box_nodes, rank_width, rank_width),
            preferred_element_type=jnp.float32,
        )
    ).astype(jnp.bfloat16)
    mid_down = jnp.einsum(
        "bsr,bjqr->bjsq",
        box_field,
        mid_up.reshape(box_nodes, 4, rank_width, rank_width),
        preferred_element_type=jnp.float32,
    )
    mid_field = (mid_far + mid_down.reshape(middle, samples, rank_width)).astype(jnp.bfloat16)
    leaf_down = jnp.einsum(
        "bsr,bjqr->bjsq",
        mid_field,
        leaf_up.reshape(middle, 4, rank_width, rank_width),
        preferred_element_type=jnp.float32,
    )
    leaf_field = (leaf_far + leaf_down.reshape(leaves, samples, rank_width)).astype(jnp.bfloat16)
    return near_field + jnp.einsum(
        "tsr,trp->tsp", leaf_field, basis, preferred_element_type=jnp.float32
    )


def solution(mesh):
    return jax.shard_map(
        body,
        mesh=mesh,
        in_specs=(
            P("leaf", None, None),
            P("leaf", None, None),
            P("leaf", None, None),
            P("leaf", None),
            P("leaf", None),
            P("leaf", None),
            P("leaf", None),
            P("leaf", None),
            P("leaf", None),
            P(),
            P("leaf", None),
            P("leaf"),
            P("leaf", None),
            P("leaf"),
            P("leaf", None),
            P("leaf"),
            P("leaf", None),
            P("leaf"),
            P(),
            P("leaf", None),
            P("leaf"),
        ),
        out_specs=P("leaf", None, None),
        check_vma=False,
    )
```

```python
import functools

import jax
import jax.numpy as jnp
from jax import lax
from jax.experimental import pallas as pl
from jax.experimental.pallas import tpu as pltpu
from jax.sharding import PartitionSpec as P


def padded(shard, sides, width):
    for axis, dim in sides:
        size, length = (lax.axis_size(axis), shard.shape[dim])
        up = [(i, (i + 1) % size) for i in range(size - 1)]
        down = [(j, i) for i, j in up]
        last = lax.slice_in_dim(shard, length - width, length, axis=dim)
        leading = lax.slice_in_dim(shard, 0, width, axis=dim)
        before = lax.ppermute(last, axis, up)
        after = lax.ppermute(leading, axis, down)
        shard = jnp.concatenate([before, shard, after], axis=dim)
    return shard


def gather_rows(block, axis):
    size = lax.axis_size(axis)
    rows = block.shape[0]
    full = jnp.zeros((rows * size,) + block.shape[1:], block.dtype)
    full = lax.dynamic_update_slice_in_dim(full, block, lax.axis_index(axis) * rows, axis=0)
    return lax.psum(full, axis)


def lift_up(coeffs, transfer, rank_width):
    nodes = coeffs.shape[0]
    matrices = transfer.reshape(nodes, rank_width, rank_width)
    return jnp.einsum("nsq,nqr->nsr", coeffs, matrices, preferred_element_type=jnp.float32)


NEG_LOG2E = -1.4426950408889634


def coupling(d2):
    return jnp.exp2((d2 * lax.rsqrt(d2)) * NEG_LOG2E).astype(jnp.bfloat16)


def nt_dot(a, b):
    return lax.dot_general(a, b, (((1,), (1,)), ((), ())), preferred_element_type=jnp.float32)


NEAR_UNROLL = 9
FAR_UNROLL = 7


def near_kernel(base_ref, src_ref, cnt_ref, vals_ref, rows_ref, tgt_ref, out_ref, *, slots):
    targets = out_ref.shape[0]
    zeros_v = jnp.zeros(vals_ref.shape[1:], vals_ref.dtype)

    def per_target(t, carry):
        frame = jnp.transpose(tgt_ref[t].astype(jnp.float32)).astype(jnp.bfloat16)
        count = cnt_ref[t]

        def step(i, acc):
            picks = [NEAR_UNROLL * i + u for u in range(NEAR_UNROLL)]
            held = [src_ref[t * slots + jnp.minimum(k, slots - 1)] for k in picks]
            d2s = [jnp.dot(frame, rows_ref[s], preferred_element_type=jnp.float32) for s in held]
            tiles = [coupling(d2) for d2 in d2s]
            for k, s, tile in zip(picks, held, tiles):
                v = jnp.where(k < count, vals_ref[s], zeros_v)
                acc = acc + nt_dot(v, tile)
            return acc

        steps = (count + NEAR_UNROLL - 1) // NEAR_UNROLL
        acc = lax.fori_loop(0, steps, step, jnp.zeros(out_ref.shape[1:], jnp.float32))
        out_ref[t] = 0.25 * acc
        return carry

    lax.fori_loop(0, targets, per_target, 0)


def far_kernel(base_ref, src_ref, cnt_ref, cd_ref, rows_ref, tgt_ref, out_ref, *, slots):
    targets, samples, rank = out_ref.shape
    width = cd_ref.shape[2]
    first_half = lax.broadcasted_iota(jnp.int32, (cd_ref.shape[1], width), 1) < rank
    zeros_c = jnp.zeros((cd_ref.shape[1], width), cd_ref.dtype)
    base = base_ref[0]

    def per_target(t, carry):
        frame = jnp.transpose(tgt_ref[base + t].astype(jnp.float32))[:rank].astype(jnp.bfloat16)
        count = cnt_ref[t]

        def source(k):
            return src_ref[t * slots + jnp.minimum(k, slots - 1)]

        def step(i, acc):
            firsts = [2 * (FAR_UNROLL * i + u) for u in range(FAR_UNROLL)]
            held = [(source(a), source(a + 1)) for a in firsts]
            d2s = [
                jnp.dot(
                    frame,
                    jnp.where(first_half, rows_ref[sa], rows_ref[sb]),
                    preferred_element_type=jnp.float32,
                )
                for sa, sb in held
            ]
            tiles = [coupling(d2) for d2 in d2s]
            for a, (sa, sb), tile in zip(firsts, held, tiles):
                ca = jnp.where(a < count, cd_ref[sa], zeros_c)
                cb = jnp.where(a + 1 < count, cd_ref[sb], zeros_c)
                acc = acc + nt_dot(jnp.where(first_half, ca, cb), tile)
            return acc

        steps = (count + 2 * FAR_UNROLL - 1) // (2 * FAR_UNROLL)
        acc = lax.fori_loop(0, steps, step, jnp.zeros((samples, rank), jnp.float32))
        out_ref[t] = 0.25 * acc
        return carry

    lax.fori_loop(0, targets, per_target, 0)


SMEM = pl.BlockSpec(memory_space=pltpu.SMEM)
VMEM = pl.BlockSpec(memory_space=pltpu.VMEM)


def bf16_split(x):
    hi = lax.reduce_precision(x, exponent_bits=8, mantissa_bits=7)
    rest = x - hi
    mid = lax.reduce_precision(rest, exponent_bits=8, mantissa_bits=7)
    return [hi, mid, rest - mid]


def source_rows(frames):
    x, y = frames[:, 0], frames[:, 1]
    one = jnp.ones_like(x)
    parts = [-2.0 * x, -2.0 * y, one, one, one] + bf16_split(x * x + y * y)
    return jnp.stack(parts, axis=1).astype(jnp.bfloat16)


def target_rows(frames):
    x, y = frames[:, 0], frames[:, 1]
    one = jnp.ones_like(x)
    parts = [x, y] + bf16_split(x * x + y * y + 0.0025) + [one, one, one]
    return jnp.stack(parts, axis=1).astype(jnp.bfloat16)


def near_sum(base, src, counts, vals, rows, tgt):
    targets, slots = src.shape
    samples, width = vals.shape[1], vals.shape[2]
    tile = width * width
    pairs = targets * slots
    return pl.pallas_call(
        functools.partial(near_kernel, slots=slots),
        out_shape=jax.ShapeDtypeStruct((targets, samples, width), jnp.float32),
        in_specs=[SMEM, SMEM, SMEM, VMEM, VMEM, VMEM],
        out_specs=VMEM,
        compiler_params=pltpu.CompilerParams(vmem_limit_bytes=48 * 1024 * 1024),
        cost_estimate=pl.CostEstimate(
            flops=pairs * (2 * (samples + 8) * tile + 3 * tile),
            transcendentals=pairs * 2 * tile,
            bytes_accessed=vals.size * 2 + rows.size * 2 + targets * samples * width * 4,
        ),
    )(base, src.reshape(-1), counts, vals, rows, tgt)


def far_sum(base, src, counts, cd, rows, tgt, rank):
    targets, slots = src.shape
    samples, width = cd.shape[1], cd.shape[2]
    tile = rank * width
    pairs = targets * (slots + 1) // 2
    return pl.pallas_call(
        functools.partial(far_kernel, slots=slots),
        out_shape=jax.ShapeDtypeStruct((targets, samples, rank), jnp.float32),
        in_specs=[SMEM, SMEM, SMEM, VMEM, VMEM, VMEM],
        out_specs=VMEM,
        compiler_params=pltpu.CompilerParams(vmem_limit_bytes=48 * 1024 * 1024),
        cost_estimate=pl.CostEstimate(
            flops=pairs * (2 * (samples + 8) * tile + 3 * tile),
            transcendentals=pairs * 2 * tile,
            bytes_accessed=cd.size * 2 + rows.size * 4 + targets * samples * rank * 4,
        ),
    )(base, src.reshape(-1), counts, cd, rows, tgt)


def far_tables(coef, skel, rank, own=None):
    cd = jnp.concatenate([coef, coef], axis=2)
    frames = skel.astype(jnp.float32).reshape(skel.shape[0], 2, rank)
    rows = source_rows(frames)
    if own is None:
        tgt = target_rows(frames)
    else:
        tgt = target_rows(own.astype(jnp.float32).reshape(own.shape[0], 2, rank))
    return cd, jnp.concatenate([rows, rows], axis=2), jnp.concatenate([tgt, tgt], axis=2)


def body(
    values,
    points,
    basis,
    leaf_up,
    mid_up,
    box_up,
    leaf_skel,
    mid_skel,
    box_skel,
    top_skel,
    near_src,
    near_count,
    leaf_src,
    leaf_count,
    mid_src,
    mid_count,
    box_src,
    box_count,
    box_parent,
    top_src,
    top_count,
):
    leaves = values.shape[0]
    samples = values.shape[1]
    rank_width = basis.shape[1]
    middle = leaves // 4
    box_nodes = leaves // 16
    top_nodes = top_count.shape[0]
    top_all = top_skel.shape[0]
    device = lax.axis_index("leaf")

    near_vals = padded(values, (("leaf", 0),), leaves)
    near_pts = padded(points, (("leaf", 0),), leaves).astype(jnp.float32)
    near_rows = near_src - (device - 1) * leaves
    near_field = near_sum(
        jnp.full((1,), leaves, jnp.int32),
        near_rows,
        near_count,
        near_vals,
        source_rows(near_pts),
        target_rows(points.astype(jnp.float32)),
    )

    leaf_coef = jnp.einsum(
        "tsp,trp->tsr", values, basis, preferred_element_type=jnp.float32
    ).astype(jnp.bfloat16)
    mid_coef = (
        lift_up(leaf_coef, leaf_up, rank_width)
        .reshape(middle, 4, samples, rank_width)
        .sum(axis=1)
        .astype(jnp.bfloat16)
    )
    box_coef = (
        lift_up(mid_coef, mid_up, rank_width)
        .reshape(box_nodes, 4, samples, rank_width)
        .sum(axis=1)
        .astype(jnp.bfloat16)
    )
    box_term = lift_up(box_coef, box_up, rank_width).astype(jnp.bfloat16)
    group_term = (
        box_term.astype(jnp.float32)
        .reshape(box_nodes // 4, 4, samples * rank_width)
        .sum(axis=1)
        .astype(jnp.bfloat16)
    )
    all_groups = gather_rows(group_term, "leaf")
    group_parent = box_parent.reshape(-1, 4)[:, 0]
    select = (
        group_parent[None, :] == jnp.arange(top_all, dtype=jnp.int32)[:, None]
    ).astype(jnp.bfloat16)
    top_coef = jnp.dot(select, all_groups, preferred_element_type=jnp.float32).astype(
        jnp.bfloat16
    )

    def pack(coef, skel):
        return jnp.concatenate([coef.reshape(coef.shape[0], -1), skel], axis=1)

    all_nodes = jnp.concatenate(
        [pack(leaf_coef, leaf_skel), pack(mid_coef, mid_skel), pack(box_coef, box_skel)], axis=0
    )
    per_device = leaves + middle + box_nodes
    node_table = padded(all_nodes, (("leaf", 0),), per_device).reshape(3, per_device, -1)
    coef_width = samples * rank_width

    def level(start, nodes, skel, src, counts):
        rows = node_table[:, start : start + nodes].reshape(3 * nodes, -1)
        coef = rows[:, :coef_width].reshape(3 * nodes, samples, rank_width)
        cd, rows_s, rows_t = far_tables(coef, rows[:, coef_width:], rank_width, skel)
        local = src - (device - 1) * nodes
        return far_sum(jnp.zeros((1,), jnp.int32), local, counts, cd, rows_s, rows_t, rank_width)

    leaf_far = level(0, leaves, leaf_skel, leaf_src, leaf_count)
    mid_far = level(leaves, middle, mid_skel, mid_src, mid_count)
    box_far = level(leaves + middle, box_nodes, box_skel, box_src, box_count)

    top_cd, top_rows, top_tgt = far_tables(
        top_coef.reshape(top_all, samples, rank_width), top_skel, rank_width
    )
    own_field = far_sum(
        (device * top_nodes).astype(jnp.int32).reshape(1),
        top_src,
        top_count,
        top_cd,
        top_rows,
        top_tgt,
        rank_width,
    ).astype(jnp.bfloat16)
    top_field = gather_rows(own_field.reshape(top_nodes, samples * rank_width), "leaf")
    own_parent = lax.dynamic_slice_in_dim(box_parent, device * box_nodes, box_nodes)
    parent_field = top_field[own_parent].reshape(box_nodes, samples, rank_width)
    box_field = (
        box_far
        + jnp.einsum(
            "bsr,bqr->bsq",
            parent_field,
            box_up.reshape(box_nodes, rank_width, rank_width),
            preferred_element_type=jnp.float32,
        )
    ).astype(jnp.bfloat16)
    mid_down = jnp.einsum(
        "bsr,bjqr->bjsq",
        box_field,
        mid_up.reshape(box_nodes, 4, rank_width, rank_width),
        preferred_element_type=jnp.float32,
    )
    mid_field = (mid_far + mid_down.reshape(middle, samples, rank_width)).astype(jnp.bfloat16)
    leaf_down = jnp.einsum(
        "bsr,bjqr->bjsq",
        mid_field,
        leaf_up.reshape(middle, 4, rank_width, rank_width),
        preferred_element_type=jnp.float32,
    )
    leaf_field = (leaf_far + leaf_down.reshape(leaves, samples, rank_width)).astype(jnp.bfloat16)
    return near_field + jnp.einsum(
        "tsr,trp->tsp", leaf_field, basis, preferred_element_type=jnp.float32
    )


def solution(mesh):
    return jax.shard_map(
        body,
        mesh=mesh,
        in_specs=(
            P("leaf", None, None),
            P("leaf", None, None),
            P("leaf", None, None),
            P("leaf", None),
            P("leaf", None),
            P("leaf", None),
            P("leaf", None),
            P("leaf", None),
            P("leaf", None),
            P(),
            P("leaf", None),
            P("leaf"),
            P("leaf", None),
            P("leaf"),
            P("leaf", None),
            P("leaf"),
            P("leaf", None),
            P("leaf"),
            P(),
            P("leaf", None),
            P("leaf"),
        ),
        out_specs=P("leaf", None, None),
        check_vma=False,
    )
```

```python
import functools

import jax
import jax.numpy as jnp
from jax import lax
from jax.experimental import pallas as pl
from jax.experimental.pallas import tpu as pltpu
from jax.sharding import PartitionSpec as P


def padded(shard, sides, width):
    for axis, dim in sides:
        size, length = (lax.axis_size(axis), shard.shape[dim])
        up = [(i, (i + 1) % size) for i in range(size - 1)]
        down = [(j, i) for i, j in up]
        last = lax.slice_in_dim(shard, length - width, length, axis=dim)
        leading = lax.slice_in_dim(shard, 0, width, axis=dim)
        before = lax.ppermute(last, axis, up)
        after = lax.ppermute(leading, axis, down)
        shard = jnp.concatenate([before, shard, after], axis=dim)
    return shard


def gather_rows(block, axis):
    size = lax.axis_size(axis)
    rows = block.shape[0]
    full = jnp.zeros((rows * size,) + block.shape[1:], block.dtype)
    full = lax.dynamic_update_slice_in_dim(full, block, lax.axis_index(axis) * rows, axis=0)
    return lax.psum(full, axis)


def lift_up(coeffs, transfer, rank_width):
    nodes = coeffs.shape[0]
    matrices = transfer.reshape(nodes, rank_width, rank_width)
    return jnp.einsum("nsq,nqr->nsr", coeffs, matrices, preferred_element_type=jnp.float32)


NEG_LOG2E = -1.4426950408889634


def coupling(d2):
    return jnp.exp2((d2 * lax.rsqrt(d2)) * NEG_LOG2E).astype(jnp.bfloat16)


def nt_dot(a, b):
    return lax.dot_general(a, b, (((1,), (1,)), ((), ())), preferred_element_type=jnp.float32)


NEAR_UNROLL = 9
FAR_UNROLL = 7


def near_kernel(base_ref, src_ref, cnt_ref, vals_ref, rows_ref, tgt_ref, out_ref, *, slots):
    targets = out_ref.shape[0]
    zeros_v = jnp.zeros(vals_ref.shape[1:], vals_ref.dtype)

    def per_target(t, carry):
        frame = jnp.transpose(tgt_ref[t].astype(jnp.float32)).astype(jnp.bfloat16)
        count = cnt_ref[t]

        def step(i, acc):
            picks = [NEAR_UNROLL * i + u for u in range(NEAR_UNROLL)]
            held = [src_ref[t * slots + jnp.minimum(k, slots - 1)] for k in picks]
            d2s = [jnp.dot(frame, rows_ref[s], preferred_element_type=jnp.float32) for s in held]
            tiles = [coupling(d2) for d2 in d2s]
            for k, s, tile in zip(picks, held, tiles):
                v = jnp.where(k < count, vals_ref[s], zeros_v)
                acc = acc + nt_dot(v, tile)
            return acc

        steps = (count + NEAR_UNROLL - 1) // NEAR_UNROLL
        acc = lax.fori_loop(0, steps, step, jnp.zeros(out_ref.shape[1:], jnp.float32))
        out_ref[t] = 0.25 * acc
        return carry

    lax.fori_loop(0, targets, per_target, 0)


def far_kernel(base_ref, src_ref, cnt_ref, cd_ref, rows_ref, tgt_ref, out_ref, *, slots):
    targets, samples, rank = out_ref.shape
    width = cd_ref.shape[2]
    first_half = lax.broadcasted_iota(jnp.int32, (cd_ref.shape[1], width), 1) < rank
    zeros_c = jnp.zeros((cd_ref.shape[1], width), cd_ref.dtype)
    base = base_ref[0]

    def per_target(t, carry):
        frame = jnp.transpose(tgt_ref[base + t].astype(jnp.float32))[:rank].astype(jnp.bfloat16)
        count = cnt_ref[t]

        def source(k):
            return src_ref[t * slots + jnp.minimum(k, slots - 1)]

        def step(i, acc):
            firsts = [2 * (FAR_UNROLL * i + u) for u in range(FAR_UNROLL)]
            held = [(source(a), source(a + 1)) for a in firsts]
            d2s = [
                jnp.dot(
                    frame,
                    jnp.where(first_half, rows_ref[sa], rows_ref[sb]),
                    preferred_element_type=jnp.float32,
                )
                for sa, sb in held
            ]
            tiles = [coupling(d2) for d2 in d2s]
            for a, (sa, sb), tile in zip(firsts, held, tiles):
                ca = jnp.where(a < count, cd_ref[sa], zeros_c)
                cb = jnp.where(a + 1 < count, cd_ref[sb], zeros_c)
                acc = acc + nt_dot(jnp.where(first_half, ca, cb), tile)
            return acc

        steps = (count + 2 * FAR_UNROLL - 1) // (2 * FAR_UNROLL)
        acc = lax.fori_loop(0, steps, step, jnp.zeros((samples, rank), jnp.float32))
        out_ref[t] = 0.25 * acc
        return carry

    lax.fori_loop(0, targets, per_target, 0)


SMEM = pl.BlockSpec(memory_space=pltpu.SMEM)
VMEM = pl.BlockSpec(memory_space=pltpu.VMEM)


def bf16_split(x):
    hi = lax.reduce_precision(x, exponent_bits=8, mantissa_bits=7)
    rest = x - hi
    mid = lax.reduce_precision(rest, exponent_bits=8, mantissa_bits=7)
    return [hi, mid, rest - mid]


def source_rows(frames):
    x, y = frames[:, 0], frames[:, 1]
    one = jnp.ones_like(x)
    parts = [-2.0 * x, -2.0 * y, one, one, one] + bf16_split(x * x + y * y)
    return jnp.stack(parts, axis=1).astype(jnp.bfloat16)


def target_rows(frames):
    x, y = frames[:, 0], frames[:, 1]
    one = jnp.ones_like(x)
    parts = [x, y] + bf16_split(x * x + y * y + 0.0025) + [one, one, one]
    return jnp.stack(parts, axis=1).astype(jnp.bfloat16)


def near_sum(base, src, counts, vals, rows, tgt):
    targets, slots = src.shape
    samples, width = vals.shape[1], vals.shape[2]
    tile = width * width
    pairs = targets * slots
    return pl.pallas_call(
        functools.partial(near_kernel, slots=slots),
        out_shape=jax.ShapeDtypeStruct((targets, samples, width), jnp.float32),
        in_specs=[SMEM, SMEM, SMEM, VMEM, VMEM, VMEM],
        out_specs=VMEM,
        compiler_params=pltpu.CompilerParams(vmem_limit_bytes=48 * 1024 * 1024),
        cost_estimate=pl.CostEstimate(
            flops=pairs * (2 * (samples + 8) * tile + 3 * tile),
            transcendentals=pairs * 2 * tile,
            bytes_accessed=vals.size * 2 + rows.size * 2 + targets * samples * width * 4,
        ),
    )(base, src.reshape(-1), counts, vals, rows, tgt)


def far_sum(base, src, counts, cd, rows, tgt, rank):
    targets, slots = src.shape
    samples, width = cd.shape[1], cd.shape[2]
    tile = rank * width
    pairs = targets * (slots + 1) // 2
    return pl.pallas_call(
        functools.partial(far_kernel, slots=slots),
        out_shape=jax.ShapeDtypeStruct((targets, samples, rank), jnp.float32),
        in_specs=[SMEM, SMEM, SMEM, VMEM, VMEM, VMEM],
        out_specs=VMEM,
        compiler_params=pltpu.CompilerParams(vmem_limit_bytes=48 * 1024 * 1024),
        cost_estimate=pl.CostEstimate(
            flops=pairs * (2 * (samples + 8) * tile + 3 * tile),
            transcendentals=pairs * 2 * tile,
            bytes_accessed=cd.size * 2 + rows.size * 4 + targets * samples * rank * 4,
        ),
    )(base, src.reshape(-1), counts, cd, rows, tgt)


def far_tables(coef, skel, rank):
    cd = jnp.concatenate([coef, coef], axis=2)
    frames = skel.astype(jnp.float32).reshape(skel.shape[0], 2, rank)
    rows = source_rows(frames)
    tgt = target_rows(frames)
    return cd, jnp.concatenate([rows, rows], axis=2), jnp.concatenate([tgt, tgt], axis=2)


def body(
    values,
    points,
    basis,
    leaf_up,
    mid_up,
    box_up,
    leaf_skel,
    mid_skel,
    box_skel,
    top_skel,
    near_src,
    near_count,
    leaf_src,
    leaf_count,
    mid_src,
    mid_count,
    box_src,
    box_count,
    box_parent,
    top_src,
    top_count,
):
    leaves = values.shape[0]
    samples = values.shape[1]
    rank_width = basis.shape[1]
    middle = leaves // 4
    box_nodes = leaves // 16
    top_nodes = top_count.shape[0]
    top_all = top_skel.shape[0]
    device = lax.axis_index("leaf")

    near_vals = padded(values, (("leaf", 0),), leaves)
    near_pts = padded(points, (("leaf", 0),), leaves).astype(jnp.float32)
    near_rows = near_src - (device - 1) * leaves
    near_field = near_sum(
        jnp.full((1,), leaves, jnp.int32),
        near_rows,
        near_count,
        near_vals,
        source_rows(near_pts),
        target_rows(points.astype(jnp.float32)),
    )

    leaf_coef = jnp.einsum(
        "tsp,trp->tsr", values, basis, preferred_element_type=jnp.float32
    ).astype(jnp.bfloat16)
    mid_coef = (
        lift_up(leaf_coef, leaf_up, rank_width)
        .reshape(middle, 4, samples, rank_width)
        .sum(axis=1)
        .astype(jnp.bfloat16)
    )
    box_coef = (
        lift_up(mid_coef, mid_up, rank_width)
        .reshape(box_nodes, 4, samples, rank_width)
        .sum(axis=1)
        .astype(jnp.bfloat16)
    )
    box_term = lift_up(box_coef, box_up, rank_width).astype(jnp.bfloat16)
    group_term = (
        box_term.astype(jnp.float32)
        .reshape(box_nodes // 4, 4, samples * rank_width)
        .sum(axis=1)
        .astype(jnp.bfloat16)
    )
    all_groups = gather_rows(group_term, "leaf")
    group_parent = box_parent.reshape(-1, 4)[:, 0]
    select = (
        group_parent[None, :] == jnp.arange(top_all, dtype=jnp.int32)[:, None]
    ).astype(jnp.bfloat16)
    top_coef = jnp.dot(select, all_groups, preferred_element_type=jnp.float32).astype(
        jnp.bfloat16
    )

    def pack(coef, skel):
        return jnp.concatenate([coef.reshape(coef.shape[0], -1), skel], axis=1)

    all_nodes = jnp.concatenate(
        [pack(leaf_coef, leaf_skel), pack(mid_coef, mid_skel), pack(box_coef, box_skel)], axis=0
    )
    per_device = leaves + middle + box_nodes
    node_table = padded(all_nodes, (("leaf", 0),), per_device).reshape(3, per_device, -1)
    coef_width = samples * rank_width

    def level(start, nodes, src, counts):
        rows = node_table[:, start : start + nodes].reshape(3 * nodes, -1)
        coef = rows[:, :coef_width].reshape(3 * nodes, samples, rank_width)
        cd, rows_s, rows_t = far_tables(coef, rows[:, coef_width:], rank_width)
        local = src - (device - 1) * nodes
        return far_sum(jnp.full((1,), nodes, jnp.int32), local, counts, cd, rows_s, rows_t, rank_width)

    leaf_far = level(0, leaves, leaf_src, leaf_count)
    mid_far = level(leaves, middle, mid_src, mid_count)
    box_far = level(leaves + middle, box_nodes, box_src, box_count)

    top_cd, top_rows, top_tgt = far_tables(
        top_coef.reshape(top_all, samples, rank_width), top_skel, rank_width
    )
    own_field = far_sum(
        (device * top_nodes).astype(jnp.int32).reshape(1),
        top_src,
        top_count,
        top_cd,
        top_rows,
        top_tgt,
        rank_width,
    ).astype(jnp.bfloat16)
    top_field = gather_rows(own_field.reshape(top_nodes, samples * rank_width), "leaf")
    own_parent = lax.dynamic_slice_in_dim(box_parent, device * box_nodes, box_nodes)
    parent_field = top_field[own_parent].reshape(box_nodes, samples, rank_width)
    box_field = (
        box_far
        + jnp.einsum(
            "bsr,bqr->bsq",
            parent_field,
            box_up.reshape(box_nodes, rank_width, rank_width),
            preferred_element_type=jnp.float32,
        )
    ).astype(jnp.bfloat16)
    mid_down = jnp.einsum(
        "bsr,bjqr->bjsq",
        box_field,
        mid_up.reshape(box_nodes, 4, rank_width, rank_width),
        preferred_element_type=jnp.float32,
    )
    mid_field = (mid_far + mid_down.reshape(middle, samples, rank_width)).astype(jnp.bfloat16)
    leaf_down = jnp.einsum(
        "bsr,bjqr->bjsq",
        mid_field,
        leaf_up.reshape(middle, 4, rank_width, rank_width),
        preferred_element_type=jnp.float32,
    )
    leaf_field = (leaf_far + leaf_down.reshape(leaves, samples, rank_width)).astype(jnp.bfloat16)
    return near_field + jnp.einsum(
        "tsr,trp->tsp", leaf_field, basis, preferred_element_type=jnp.float32
    )


def solution(mesh):
    return jax.shard_map(
        body,
        mesh=mesh,
        in_specs=(
            P("leaf", None, None),
            P("leaf", None, None),
            P("leaf", None, None),
            P("leaf", None),
            P("leaf", None),
            P("leaf", None),
            P("leaf", None),
            P("leaf", None),
            P("leaf", None),
            P(),
            P("leaf", None),
            P("leaf"),
            P("leaf", None),
            P("leaf"),
            P("leaf", None),
            P("leaf"),
            P("leaf", None),
            P("leaf"),
            P(),
            P("leaf", None),
            P("leaf"),
        ),
        out_specs=P("leaf", None, None),
        check_vma=False,
    )
```
